32 devices in a mesh: illum: 8 (over z, y), tile: 4 (over x, core).
Axes of the slice: x: 2, y: 2, z: 4, core: 2. Of those that a mesh axis runs over, the one named last changes fastest.
Arguments:
- tilts: int32 [8, 2], P('illum'), may hold values from -64 to 64
- taps: float32 [2, 33], replicated, may hold values from -0.75 to 0.75
- stored_planes: float32 [2, 128, 4096], P(None, 'tile', 'illum'), may hold values from -3.140625 to 3.140625
- owner: int32 [2, 8], replicated, may hold values from 0 to 7, each once within a row
Outputs:
- exit_field: float32 [2, 8, 128, 4096], P(None, 'illum', 'tile')
The draws below stay inside these ranges and needn't reach their ends.
Inputs may be any that keep to these rules, and one draw needn't show every extreme that they name: Each row of owner is a permutation of the 8 stored column blocks.
All inputs are finite; a program needn't handle non-finite values.
Results may differ from the reference program's by a relative error of at most 0.0003.
Values sent between devices are 32-bit elements; how exact they have to be, the bound alone decides.
No kernel may reach another device: no remote copies, remote signals or barrier semaphores. Data moves between devices by JAX's collectives and lax.ppermute only.
A program may use at most 64 MiB of HBM per device.

```python
import jax
import jax.numpy as jnp
from jax import lax

NY = 4096
PLANES = 2
HALF = 16
TAPS = 33
NX = 128
ILLUMS = 8
N_ILLUM = 8


def touch_ends(values, own_key, least, largest):
    longest = values.shape.index(max(values.shape))
    spots = []
    for shift in (0, 1):
        where = [jax.random.randint(jax.random.fold_in(own_key, axis), (), 0, length) for axis, length in enumerate(values.shape)]
        where[longest] = (where[longest] + shift) % values.shape[longest]
        spots.append(tuple(where))
    return values.at[spots[0]].set(least).at[spots[1]].set(largest)


def centred(key, shape, scale, bound, held_as=jnp.bfloat16):
    values = scale * jax.random.normal(key, shape, jnp.float32)
    return jnp.clip(values, min=-bound, max=bound).astype(held_as)


def setup_inputs(seed: int = 0) -> dict:
    arg_keys = jax.random.split(jax.random.key(seed), 5)
    tilts = touch_ends(jax.random.randint(arg_keys[0], (ILLUMS, 2), -64, 65), jax.random.fold_in(arg_keys[0], 1), -64, 64).astype(jnp.int32)
    taps = centred(arg_keys[1], (2, TAPS), (2 * TAPS) ** -0.5, 0.75, jnp.float32)
    stored_planes = jnp.clip(jax.random.uniform(arg_keys[2], (PLANES, NX, NY), jnp.float32, -3.140625, 3.140625), -3.140625, 3.140625)
    owner = jax.vmap(lambda own: jax.random.permutation(own, N_ILLUM))(jax.random.split(arg_keys[3], PLANES)).reshape((PLANES, N_ILLUM)).astype(jnp.int32)
    return {"tilts": tilts, "taps": taps, "stored_planes": stored_planes, "owner": owner}


two_pi = 6.283185307179586


def toeplitz(tap_row, block):
    rows = jnp.arange(block + 2 * HALF)[:, None]
    cols = jnp.arange(block)[None, :]
    offset = rows - cols
    steps = jnp.arange(2 * HALF + 1)
    return jnp.sum(jnp.where(offset[:, :, None] == steps, tap_row, 0.0), axis=2)


def windows(field, block):
    length = field.shape[-1]
    count = length // block
    widths = [(0, 0)] * (field.ndim - 1) + [(HALF, block - HALF)]
    padded = jnp.pad(field, widths)
    lead = field.shape[:-1]
    main = padded[..., :length].reshape(lead + (count, block))
    after = padded[..., block:length + block].reshape(lead + (count, block))[..., :2 * HALF]
    return jnp.concatenate([main, after], axis=-1)


def conv_last(real, imag, taps):
    block = min(128, real.shape[-1])
    win_real = windows(real, block)
    win_imag = windows(imag, block)
    kern_real = toeplitz(taps[0], block)
    kern_imag = toeplitz(taps[1], block)

    def apply(win, kern):
        out = jnp.einsum("...nj,jc->...nc", win, kern, precision=lax.Precision.HIGHEST)
        return out.reshape(real.shape)

    return (apply(win_real, kern_real) - apply(win_imag, kern_imag),
            apply(win_real, kern_imag) + apply(win_imag, kern_real))


def reference(tilts, taps, stored_planes, owner):
    width = NY // N_ILLUM
    screens = jnp.stack([stored_planes[p].reshape(NX, N_ILLUM, width)[:, owner[p], :].reshape(NX, NY) for p in range(PLANES)])
    rows = jnp.arange(NX, dtype=jnp.int32)
    cols = jnp.arange(NY, dtype=jnp.int32)

    def one(tilt):
        across = jnp.mod(tilt[0] * rows, NX).astype(jnp.float32) / NX
        along = jnp.mod(tilt[1] * cols, NY).astype(jnp.float32) / NY
        theta = two_pi * (across[:, None] + along[None, :])
        real = jnp.cos(theta)
        imag = jnp.sin(theta)
        for p in range(PLANES):
            cosine = jnp.cos(screens[p])
            sine = jnp.sin(screens[p])
            real, imag = real * cosine - imag * sine, real * sine + imag * cosine
            real_t, imag_t = conv_last(real.T, imag.T, taps)
            real, imag = conv_last(real_t.T, imag_t.T, taps)
        return jnp.stack([real, imag])

    result = lax.map(one, tilts)
    return jnp.transpose(result, (1, 0, 2, 3))
```

```python
import jax
import jax.numpy as jnp
from jax import lax
from jax.sharding import PartitionSpec as P

NY = 4096
PLANES = 2
HALF = 16


two_pi = 6.283185307179586


def extended(cells, sides, width):
    for axis, dim in sides:
        count = lax.axis_size(axis)
        ends = count - 1
        head = lax.slice_in_dim(cells, 0, width, axis=dim)
        tail = lax.slice_in_dim(cells, cells.shape[dim] - width, cells.shape[dim], axis=dim)
        cells = jnp.concatenate(
            [
                lax.ppermute(tail, axis, [(i, (i + 1) % count) for i in range(ends)]),
                cells,
                lax.ppermute(head, axis, [((i + 1) % count, i) for i in range(ends)]),
            ],
            axis=dim,
        )
    return cells


def toeplitz(tap_row, block):
    rows = jnp.arange(block + 2 * HALF)[:, None]
    cols = jnp.arange(block)[None, :]
    offset = rows - cols
    steps = jnp.arange(2 * HALF + 1)
    return jnp.sum(jnp.where(offset[:, :, None] == steps, tap_row, 0.0), axis=2)


def band_matrix(tap_row, count):
    rows = jnp.arange(count)[:, None]
    cols = jnp.arange(count + 2 * HALF)[None, :]
    offset = cols - rows
    steps = jnp.arange(2 * HALF + 1)
    return jnp.sum(jnp.where(offset[:, :, None] == steps, tap_row, 0.0), axis=2)


def windows(field, block):
    length = field.shape[-1]
    count = length // block
    widths = [(0, 0)] * (field.ndim - 1) + [(HALF, block - HALF)]
    padded = jnp.pad(field, widths)
    lead = field.shape[:-1]
    main = padded[..., :length].reshape(lead + (count, block))
    after = padded[..., block : length + block].reshape(lead + (count, block))[..., : 2 * HALF]
    return jnp.concatenate([main, after], axis=-1)


def along_pass(real, imag, taps):
    block = min(128, real.shape[-1])
    win_real = windows(real, block)
    win_imag = windows(imag, block)
    kern_real = toeplitz(taps[0], block)
    kern_imag = toeplitz(taps[1], block)

    def apply(win, kern):
        out = jnp.einsum("...nj,jc->...nc", win, kern, precision=lax.Precision.HIGHEST)
        return out.reshape(real.shape)

    return (
        apply(win_real, kern_real) - apply(win_imag, kern_imag),
        apply(win_real, kern_imag) + apply(win_imag, kern_real),
    )


def cross_pass(real, imag, taps):
    count = real.shape[1] - 2 * HALF
    band_real = band_matrix(taps[0], count)
    band_imag = band_matrix(taps[1], count)

    def apply(band, field):
        return jnp.einsum("ij,ajy->aiy", band, field, precision=lax.Precision.HIGHEST)

    return (
        apply(band_real, real) - apply(band_imag, imag),
        apply(band_real, imag) + apply(band_imag, real),
    )


def transmit(real, imag, screen):
    cosine = jnp.cos(screen)
    sine = jnp.sin(screen)
    return (real * cosine - imag * sine, real * sine + imag * cosine)


def reorder(gathered, owner):
    count = gathered.shape[1]
    blocks = owner.shape[1]
    width = gathered.shape[2] // blocks
    planes = [
        gathered[p].reshape(count, blocks, width)[:, owner[p], :].reshape(count, blocks * width)
        for p in range(gathered.shape[0])
    ]
    return jnp.stack(planes)


def gather_screens(stored_planes, owner, axis):
    count = lax.axis_size(axis)
    me = lax.axis_index(axis)
    parts = [stored_planes]
    for shift in range(1, count):
        parts.append(lax.ppermute(stored_planes, axis, [(i, (i + shift) % count) for i in range(count)]))
    stacked = jnp.stack(parts, axis=1)
    rows = stored_planes.shape[1]
    width = stored_planes.shape[2]
    planes = []
    for p in range(stored_planes.shape[0]):
        picked = stacked[p][jnp.mod(me - owner[p], count)]
        planes.append(jnp.transpose(picked, (1, 0, 2)).reshape(rows, count * width))
    return jnp.stack(planes)


def body(tilts, taps, stored_planes, owner):
    local_rows = stored_planes.shape[1]
    total_rows = local_rows * lax.axis_size("tile")
    total_cols = NY
    first_row = lax.axis_index("tile") * local_rows
    screens = gather_screens(stored_planes, owner, "illum")
    extra = 0
    span = local_rows + 2 * extra
    global_rows = first_row - extra + jnp.arange(span, dtype=jnp.int32)
    inside = (global_rows >= 0) & (global_rows < total_rows)
    cols = jnp.arange(total_cols, dtype=jnp.int32)
    across = (
        jnp.mod(tilts[:, 0:1] * global_rows[None, :], total_rows).astype(jnp.float32) / total_rows
    )
    along = jnp.mod(tilts[:, 1:2] * cols[None, :], total_cols).astype(jnp.float32) / total_cols
    theta = two_pi * (across[:, :, None] + along[:, None, :])
    real = jnp.where(inside[None, :, None], jnp.cos(theta), 0.0)
    imag = jnp.where(inside[None, :, None], jnp.sin(theta), 0.0)
    for plane in range(PLANES):
        real, imag = transmit(real, imag, screens[plane])
        packed = extended(jnp.stack([real, imag]), (("tile", 2),), HALF)
        real, imag = cross_pass(packed[0], packed[1], taps)
        real, imag = along_pass(real, imag, taps)
    return jnp.stack([real, imag])


def solution(mesh):
    in_specs = (P("illum", None), P(), P(None, "tile", "illum"), P())
    out_specs = P(None, "illum", "tile", None)
    return jax.shard_map(body, mesh=mesh, in_specs=in_specs, out_specs=out_specs, check_vma=False)
```

```python
import jax
import jax.numpy as jnp
from jax import lax
from jax.sharding import PartitionSpec as P

NY = 4096
PLANES = 2
HALF = 16


two_pi = 6.283185307179586


def extended(cells, sides, width):
    for axis, dim in sides:
        count = lax.axis_size(axis)
        ends = count - 1
        head = lax.slice_in_dim(cells, 0, width, axis=dim)
        tail = lax.slice_in_dim(cells, cells.shape[dim] - width, cells.shape[dim], axis=dim)
        cells = jnp.concatenate(
            [
                lax.ppermute(tail, axis, [(i, (i + 1) % count) for i in range(ends)]),
                cells,
                lax.ppermute(head, axis, [((i + 1) % count, i) for i in range(ends)]),
            ],
            axis=dim,
        )
    return cells


def toeplitz(tap_row, block):
    rows = jnp.arange(block + 2 * HALF)[:, None]
    cols = jnp.arange(block)[None, :]
    offset = rows - cols
    steps = jnp.arange(2 * HALF + 1)
    return jnp.sum(jnp.where(offset[:, :, None] == steps, tap_row, 0.0), axis=2)


def band_matrix(tap_row, count):
    rows = jnp.arange(count)[:, None]
    cols = jnp.arange(count + 2 * HALF)[None, :]
    offset = cols - rows
    steps = jnp.arange(2 * HALF + 1)
    return jnp.sum(jnp.where(offset[:, :, None] == steps, tap_row, 0.0), axis=2)


def windows(field, block):
    length = field.shape[-1]
    count = length // block
    widths = [(0, 0)] * (field.ndim - 1) + [(HALF, block - HALF)]
    padded = jnp.pad(field, widths)
    lead = field.shape[:-1]
    main = padded[..., :length].reshape(lead + (count, block))
    after = padded[..., block : length + block].reshape(lead + (count, block))[..., : 2 * HALF]
    return jnp.concatenate([main, after], axis=-1)


def complex_stack(real_part, imag_part):
    top = jnp.concatenate([real_part, -imag_part], axis=1)
    bottom = jnp.concatenate([imag_part, real_part], axis=1)
    return jnp.concatenate([top, bottom], axis=0)


def along_pass(real, imag, taps):
    block = min(128, real.shape[-1])
    win = jnp.concatenate([windows(real, block), windows(imag, block)], axis=-1)
    kern = complex_stack(toeplitz(taps[0], block), -toeplitz(taps[1], block))
    out = jnp.einsum("...nj,jc->...nc", win, kern, precision=lax.Precision.HIGH)
    return out[..., :block].reshape(real.shape), out[..., block:].reshape(real.shape)


def cross_pass(real, imag, taps):
    count = real.shape[1] - 2 * HALF
    band = complex_stack(band_matrix(taps[0], count), band_matrix(taps[1], count))
    field = jnp.concatenate([real, imag], axis=1)
    out = jnp.einsum("ij,ajy->aiy", band, field, precision=lax.Precision.HIGH)
    return out[:, :count], out[:, count:]


def transmit(real, imag, screen):
    cosine = jnp.cos(screen)
    sine = jnp.sin(screen)
    return (real * cosine - imag * sine, real * sine + imag * cosine)


def reorder(gathered, owner):
    count = gathered.shape[1]
    blocks = owner.shape[1]
    width = gathered.shape[2] // blocks
    planes = [
        gathered[p].reshape(count, blocks, width)[:, owner[p], :].reshape(count, blocks * width)
        for p in range(gathered.shape[0])
    ]
    return jnp.stack(planes)


def gather_screens(stored_planes, owner, axis):
    count = lax.axis_size(axis)
    me = lax.axis_index(axis)
    parts = [stored_planes]
    for shift in range(1, count):
        parts.append(lax.ppermute(stored_planes, axis, [(i, (i + shift) % count) for i in range(count)]))
    stacked = jnp.stack(parts, axis=1)
    rows = stored_planes.shape[1]
    width = stored_planes.shape[2]
    planes = []
    for p in range(stored_planes.shape[0]):
        picked = stacked[p][jnp.mod(me - owner[p], count)]
        planes.append(jnp.transpose(picked, (1, 0, 2)).reshape(rows, count * width))
    return jnp.stack(planes)


def body(tilts, taps, stored_planes, owner):
    local_rows = stored_planes.shape[1]
    total_rows = local_rows * lax.axis_size("tile")
    total_cols = NY
    first_row = lax.axis_index("tile") * local_rows
    screens = gather_screens(stored_planes, owner, "illum")
    extra = 0
    span = local_rows + 2 * extra
    global_rows = first_row - extra + jnp.arange(span, dtype=jnp.int32)
    inside = (global_rows >= 0) & (global_rows < total_rows)
    cols = jnp.arange(total_cols, dtype=jnp.int32)
    across = (
        jnp.mod(tilts[:, 0:1] * global_rows[None, :], total_rows).astype(jnp.float32) / total_rows
    )
    along = jnp.mod(tilts[:, 1:2] * cols[None, :], total_cols).astype(jnp.float32) / total_cols
    theta = two_pi * (across[:, :, None] + along[:, None, :])
    real = jnp.where(inside[None, :, None], jnp.cos(theta), 0.0)
    imag = jnp.where(inside[None, :, None], jnp.sin(theta), 0.0)
    for plane in range(PLANES):
        real, imag = transmit(real, imag, screens[plane])
        packed = extended(jnp.stack([real, imag]), (("tile", 2),), HALF)
        real, imag = cross_pass(packed[0], packed[1], taps)
        real, imag = along_pass(real, imag, taps)
    return jnp.stack([real, imag])


def solution(mesh):
    in_specs = (P("illum", None), P(), P(None, "tile", "illum"), P())
    out_specs = P(None, "illum", "tile", None)
    return jax.shard_map(body, mesh=mesh, in_specs=in_specs, out_specs=out_specs, check_vma=False)
```

```python
import jax
import jax.numpy as jnp
from jax import lax
from jax.sharding import PartitionSpec as P

NY = 4096
PLANES = 2
HALF = 16


two_pi = 6.283185307179586


def extended(cells, sides, width):
    for axis, dim in sides:
        count = lax.axis_size(axis)
        ends = count - 1
        head = lax.slice_in_dim(cells, 0, width, axis=dim)
        tail = lax.slice_in_dim(cells, cells.shape[dim] - width, cells.shape[dim], axis=dim)
        cells = jnp.concatenate(
            [
                lax.ppermute(tail, axis, [(i, (i + 1) % count) for i in range(ends)]),
                cells,
                lax.ppermute(head, axis, [((i + 1) % count, i) for i in range(ends)]),
            ],
            axis=dim,
        )
    return cells


def toeplitz(tap_row, block):
    rows = jnp.arange(block + 2 * HALF)[:, None]
    cols = jnp.arange(block)[None, :]
    offset = rows - cols
    steps = jnp.arange(2 * HALF + 1)
    return jnp.sum(jnp.where(offset[:, :, None] == steps, tap_row, 0.0), axis=2)


def band_matrix(tap_row, count):
    rows = jnp.arange(count)[:, None]
    cols = jnp.arange(count + 2 * HALF)[None, :]
    offset = cols - rows
    steps = jnp.arange(2 * HALF + 1)
    return jnp.sum(jnp.where(offset[:, :, None] == steps, tap_row, 0.0), axis=2)


def windows(field, block):
    length = field.shape[-1]
    count = length // block
    widths = [(0, 0)] * (field.ndim - 1) + [(HALF, block - HALF)]
    padded = jnp.pad(field, widths)
    lead = field.shape[:-1]
    main = padded[..., :length].reshape(lead + (count, block))
    after = padded[..., block : length + block].reshape(lead + (count, block))[..., : 2 * HALF]
    return jnp.concatenate([main, after], axis=-1)


def complex_stack(real_part, imag_part):
    top = jnp.concatenate([real_part, -imag_part], axis=1)
    bottom = jnp.concatenate([imag_part, real_part], axis=1)
    return jnp.concatenate([top, bottom], axis=0)


def along_pass(real, imag, taps):
    block = min(128, real.shape[-1])
    win = jnp.concatenate([windows(real, block), windows(imag, block)], axis=-1)
    kern = complex_stack(toeplitz(taps[0], block), -toeplitz(taps[1], block))
    out = jnp.einsum("...nj,jc->...nc", win, kern, precision=lax.Precision.HIGH)
    return out[..., :block].reshape(real.shape), out[..., block:].reshape(real.shape)


def cross_pass(real, imag, taps):
    count = real.shape[1] - 2 * HALF
    band = complex_stack(band_matrix(taps[0], count), band_matrix(taps[1], count))
    field = jnp.concatenate([real, imag], axis=1)
    out = jnp.einsum("ij,ajy->aiy", band, field, precision=lax.Precision.HIGH)
    return out[:, :count], out[:, count:]


def transmit(real, imag, screen):
    cosine = jnp.cos(screen)
    sine = jnp.sin(screen)
    return (real * cosine - imag * sine, real * sine + imag * cosine)


def reorder(gathered, owner):
    count = gathered.shape[1]
    blocks = owner.shape[1]
    width = gathered.shape[2] // blocks
    planes = [
        gathered[p].reshape(count, blocks, width)[:, owner[p], :].reshape(count, blocks * width)
        for p in range(gathered.shape[0])
    ]
    return jnp.stack(planes)


def gather_screens(stored_planes, owner, axis):
    count = lax.axis_size(axis)
    me = lax.axis_index(axis)
    paired = count & (count - 1) == 0

    def partner(i, k):
        return i ^ k if paired else (i + k) % count

    parts = [stored_planes]
    for k in range(1, count):
        parts.append(lax.ppermute(stored_planes, axis, [(i, partner(i, k)) for i in range(count)]))
    stacked = jnp.stack(parts, axis=1)
    rows = stored_planes.shape[1]
    width = stored_planes.shape[2]
    planes = []
    for p in range(stored_planes.shape[0]):
        source = jnp.bitwise_xor(me, owner[p]) if paired else jnp.mod(me - owner[p], count)
        picked = stacked[p][source]
        planes.append(jnp.transpose(picked, (1, 0, 2)).reshape(rows, count * width))
    return jnp.stack(planes)


def body(tilts, taps, stored_planes, owner):
    local_rows = stored_planes.shape[1]
    total_rows = local_rows * lax.axis_size("tile")
    total_cols = NY
    first_row = lax.axis_index("tile") * local_rows
    screens = gather_screens(stored_planes, owner, "illum")
    extra = 0
    span = local_rows + 2 * extra
    global_rows = first_row - extra + jnp.arange(span, dtype=jnp.int32)
    inside = (global_rows >= 0) & (global_rows < total_rows)
    cols = jnp.arange(total_cols, dtype=jnp.int32)
    across = (
        jnp.mod(tilts[:, 0:1] * global_rows[None, :], total_rows).astype(jnp.float32) / total_rows
    )
    along = jnp.mod(tilts[:, 1:2] * cols[None, :], total_cols).astype(jnp.float32) / total_cols
    across_cos = jnp.where(inside[None, :], jnp.cos(two_pi * across), 0.0)[:, :, None]
    across_sin = jnp.where(inside[None, :], jnp.sin(two_pi * across), 0.0)[:, :, None]
    along_cos = jnp.cos(two_pi * along)[:, None, :]
    along_sin = jnp.sin(two_pi * along)[:, None, :]
    real = across_cos * along_cos - across_sin * along_sin
    imag = across_sin * along_cos + across_cos * along_sin
    for plane in range(PLANES):
        real, imag = transmit(real, imag, screens[plane])
        packed = extended(jnp.stack([real, imag]), (("tile", 2),), HALF)
        real, imag = cross_pass(packed[0], packed[1], taps)
        real, imag = along_pass(real, imag, taps)
    return jnp.stack([real, imag])


def solution(mesh):
    in_specs = (P("illum", None), P(), P(None, "tile", "illum"), P())
    out_specs = P(None, "illum", "tile", None)
    return jax.shard_map(body, mesh=mesh, in_specs=in_specs, out_specs=out_specs, check_vma=False)
```

```python
import jax
import jax.numpy as jnp
from jax import lax
from jax.sharding import PartitionSpec as P

NY = 4096
PLANES = 2
HALF = 16


two_pi = 6.283185307179586


def extended(cells, sides, width):
    for axis, dim in sides:
        count = lax.axis_size(axis)
        ends = count - 1
        head = lax.slice_in_dim(cells, 0, width, axis=dim)
        tail = lax.slice_in_dim(cells, cells.shape[dim] - width, cells.shape[dim], axis=dim)
        cells = jnp.concatenate(
            [
                lax.ppermute(tail, axis, [(i, (i + 1) % count) for i in range(ends)]),
                cells,
                lax.ppermute(head, axis, [((i + 1) % count, i) for i in range(ends)]),
            ],
            axis=dim,
        )
    return cells


def toeplitz(tap_row, block):
    rows = jnp.arange(block + 2 * HALF)[:, None]
    cols = jnp.arange(block)[None, :]
    offset = rows - cols
    steps = jnp.arange(2 * HALF + 1)
    return jnp.sum(jnp.where(offset[:, :, None] == steps, tap_row, 0.0), axis=2)


def band_matrix(tap_row, count):
    rows = jnp.arange(count)[:, None]
    cols = jnp.arange(count + 2 * HALF)[None, :]
    offset = cols - rows
    steps = jnp.arange(2 * HALF + 1)
    return jnp.sum(jnp.where(offset[:, :, None] == steps, tap_row, 0.0), axis=2)


def windows(field, block):
    length = field.shape[-1]
    count = length // block
    widths = [(0, 0)] * (field.ndim - 1) + [(HALF, block - HALF)]
    padded = jnp.pad(field, widths)
    lead = field.shape[:-1]
    main = padded[..., :length].reshape(lead + (count, block))
    after = padded[..., block : length + block].reshape(lead + (count, block))[..., : 2 * HALF]
    return jnp.concatenate([main, after], axis=-1)


def complex_stack(real_part, imag_part):
    top = jnp.concatenate([real_part, -imag_part], axis=1)
    bottom = jnp.concatenate([imag_part, real_part], axis=1)
    return jnp.concatenate([top, bottom], axis=0)


def along_pass(real, imag, taps):
    block = min(128, real.shape[-1])
    win = jnp.concatenate([windows(real, block), windows(imag, block)], axis=-1)
    kern = complex_stack(toeplitz(taps[0], block), -toeplitz(taps[1], block))
    out = jnp.einsum("...nj,jc->...nc", win, kern, precision=lax.Precision.HIGH)
    return out[..., :block].reshape(real.shape), out[..., block:].reshape(real.shape)


def cross_pass(real, imag, taps):
    count = real.shape[1] - 2 * HALF
    band = complex_stack(band_matrix(taps[0], count), band_matrix(taps[1], count))
    field = jnp.concatenate([real, imag], axis=1)
    out = jnp.einsum("ij,ajy->aiy", band, field, precision=lax.Precision.HIGH)
    return out[:, :count], out[:, count:]


def transmit(real, imag, screen):
    cosine = jnp.cos(screen)
    sine = jnp.sin(screen)
    return (real * cosine - imag * sine, real * sine + imag * cosine)


def reorder(gathered, owner):
    count = gathered.shape[1]
    blocks = owner.shape[1]
    width = gathered.shape[2] // blocks
    planes = [
        gathered[p].reshape(count, blocks, width)[:, owner[p], :].reshape(count, blocks * width)
        for p in range(gathered.shape[0])
    ]
    return jnp.stack(planes)


def gather_screens(stored_planes, owner, axis):
    count = lax.axis_size(axis)
    me = lax.axis_index(axis)
    paired = count & (count - 1) == 0

    def partner(i, k):
        return i ^ k if paired else (i + k) % count

    parts = [stored_planes]
    for k in range(1, count):
        parts.append(lax.ppermute(stored_planes, axis, [(i, partner(i, k)) for i in range(count)]))
    stacked = jnp.stack(parts, axis=1)
    rows = stored_planes.shape[1]
    width = stored_planes.shape[2]
    planes = []
    for p in range(stored_planes.shape[0]):
        source = jnp.bitwise_xor(me, owner[p]) if paired else jnp.mod(me - owner[p], count)
        picked = stacked[p][source]
        planes.append(jnp.transpose(picked, (1, 0, 2)).reshape(rows, count * width))
    return jnp.stack(planes)


def body(tilts, taps, stored_planes, owner):
    local_rows = stored_planes.shape[1]
    total_rows = local_rows * lax.axis_size("tile")
    total_cols = NY
    first_row = lax.axis_index("tile") * local_rows
    screens = gather_screens(stored_planes, owner, "illum")
    extra = HALF
    span = local_rows + 2 * extra
    global_rows = first_row - extra + jnp.arange(span, dtype=jnp.int32)
    inside = (global_rows >= 0) & (global_rows < total_rows)
    cols = jnp.arange(total_cols, dtype=jnp.int32)
    across = (
        jnp.mod(tilts[:, 0:1] * global_rows[None, :], total_rows).astype(jnp.float32) / total_rows
    )
    along = jnp.mod(tilts[:, 1:2] * cols[None, :], total_cols).astype(jnp.float32) / total_cols
    across_cos = jnp.where(inside[None, :], jnp.cos(two_pi * across), 0.0)[:, :, None]
    across_sin = jnp.where(inside[None, :], jnp.sin(two_pi * across), 0.0)[:, :, None]
    along_cos = jnp.cos(two_pi * along)[:, None, :]
    along_sin = jnp.sin(two_pi * along)[:, None, :]
    real = across_cos * along_cos - across_sin * along_sin
    imag = across_sin * along_cos + across_cos * along_sin
    halo = extended(screens[0], (("tile", 0),), HALF)
    pieces = [
        transmit(real[:, rows], imag[:, rows], screen)
        for rows, screen in (
            (slice(0, HALF), halo[:HALF]),
            (slice(HALF, HALF + local_rows), screens[0]),
            (slice(HALF + local_rows, span), halo[HALF + local_rows :]),
        )
    ]
    real = jnp.concatenate([piece[0] for piece in pieces], axis=1)
    imag = jnp.concatenate([piece[1] for piece in pieces], axis=1)
    real, imag = cross_pass(real, imag, taps)
    real, imag = along_pass(real, imag, taps)
    for plane in range(1, PLANES):
        real, imag = transmit(real, imag, screens[plane])
        packed = extended(jnp.stack([real, imag]), (("tile", 2),), HALF)
        real, imag = cross_pass(packed[0], packed[1], taps)
        real, imag = along_pass(real, imag, taps)
    return jnp.stack([real, imag])


def solution(mesh):
    in_specs = (P("illum", None), P(), P(None, "tile", "illum"), P())
    out_specs = P(None, "illum", "tile", None)
    return jax.shard_map(body, mesh=mesh, in_specs=in_specs, out_specs=out_specs, check_vma=False)
```

```python
import jax
import jax.numpy as jnp
from jax import lax
from jax.sharding import PartitionSpec as P

NY = 4096
PLANES = 2
HALF = 16


two_pi = 6.283185307179586


def extended(cells, sides, width):
    for axis, dim in sides:
        count = lax.axis_size(axis)
        ends = count - 1
        head = lax.slice_in_dim(cells, 0, width, axis=dim)
        tail = lax.slice_in_dim(cells, cells.shape[dim] - width, cells.shape[dim], axis=dim)
        cells = jnp.concatenate(
            [
                lax.ppermute(tail, axis, [(i, (i + 1) % count) for i in range(ends)]),
                cells,
                lax.ppermute(head, axis, [((i + 1) % count, i) for i in range(ends)]),
            ],
            axis=dim,
        )
    return cells


def toeplitz(tap_row, block):
    rows = jnp.arange(block + 2 * HALF)[:, None]
    cols = jnp.arange(block)[None, :]
    offset = rows - cols
    steps = jnp.arange(2 * HALF + 1)
    return jnp.sum(jnp.where(offset[:, :, None] == steps, tap_row, 0.0), axis=2)


def band_matrix(tap_row, count):
    rows = jnp.arange(count)[:, None]
    cols = jnp.arange(count + 2 * HALF)[None, :]
    offset = cols - rows
    steps = jnp.arange(2 * HALF + 1)
    return jnp.sum(jnp.where(offset[:, :, None] == steps, tap_row, 0.0), axis=2)


def windows(field, block):
    length = field.shape[-1]
    count = length // block
    widths = [(0, 0)] * (field.ndim - 1) + [(HALF, block - HALF)]
    padded = jnp.pad(field, widths)
    lead = field.shape[:-1]
    main = padded[..., :length].reshape(lead + (count, block))
    after = padded[..., block : length + block].reshape(lead + (count, block))[..., : 2 * HALF]
    return jnp.concatenate([main, after], axis=-1)


def complex_stack(real_part, imag_part):
    top = jnp.concatenate([real_part, -imag_part], axis=1)
    bottom = jnp.concatenate([imag_part, real_part], axis=1)
    return jnp.concatenate([top, bottom], axis=0)


def along_pass(real, imag, taps):
    block = min(128, real.shape[-1])
    win = jnp.concatenate([windows(real, block), windows(imag, block)], axis=-1)
    kern = complex_stack(toeplitz(taps[0], block), -toeplitz(taps[1], block))
    out = jnp.einsum("...nj,jc->...nc", win, kern, precision=lax.Precision.HIGH)
    return out[..., :block].reshape(real.shape), out[..., block:].reshape(real.shape)


def cross_pass(real, imag, taps):
    count = real.shape[1] - 2 * HALF
    band = complex_stack(band_matrix(taps[0], count), band_matrix(taps[1], count))
    field = jnp.concatenate([real, imag], axis=1)
    out = jnp.einsum("ij,ajy->aiy", band, field, precision=lax.Precision.HIGH)
    return out[:, :count], out[:, count:]


def transmit(real, imag, screen):
    cosine = jnp.cos(screen)
    sine = jnp.sin(screen)
    return (real * cosine - imag * sine, real * sine + imag * cosine)


def reorder(gathered, owner):
    count = gathered.shape[1]
    blocks = owner.shape[1]
    width = gathered.shape[2] // blocks
    planes = [
        gathered[p].reshape(count, blocks, width)[:, owner[p], :].reshape(count, blocks * width)
        for p in range(gathered.shape[0])
    ]
    return jnp.stack(planes)


def gather_screens(stored_planes, owner, axis):
    count = lax.axis_size(axis)
    me = lax.axis_index(axis)
    paired = count & (count - 1) == 0

    def partner(i, k):
        return i ^ k if paired else (i + k) % count

    parts = [stored_planes]
    for k in range(1, count):
        parts.append(lax.ppermute(stored_planes, axis, [(i, partner(i, k)) for i in range(count)]))
    stacked = jnp.stack(parts, axis=1)
    rows = stored_planes.shape[1]
    width = stored_planes.shape[2]
    planes = []
    for p in range(stored_planes.shape[0]):
        source = jnp.bitwise_xor(me, owner[p]) if paired else jnp.mod(me - owner[p], count)
        picked = stacked[p][source]
        planes.append(jnp.transpose(picked, (1, 0, 2)).reshape(rows, count * width))
    return jnp.stack(planes)


def body(tilts, taps, stored_planes, owner):
    local_rows = stored_planes.shape[1]
    total_rows = local_rows * lax.axis_size("tile")
    total_cols = NY
    first_row = lax.axis_index("tile") * local_rows
    screens = gather_screens(stored_planes, owner, "illum")
    extra = HALF
    span = local_rows + 2 * extra
    global_rows = first_row - extra + jnp.arange(span, dtype=jnp.int32)
    inside = (global_rows >= 0) & (global_rows < total_rows)
    cols = jnp.arange(total_cols, dtype=jnp.int32)
    across = (
        jnp.mod(tilts[:, 0:1] * global_rows[None, :], total_rows).astype(jnp.float32) / total_rows
    )
    along = jnp.mod(tilts[:, 1:2] * cols[None, :], total_cols).astype(jnp.float32) / total_cols
    across_cos = jnp.where(inside[None, :], jnp.cos(two_pi * across), 0.0)[:, :, None]
    across_sin = jnp.where(inside[None, :], jnp.sin(two_pi * across), 0.0)[:, :, None]
    along_cos = jnp.cos(two_pi * along)[:, None, :]
    along_sin = jnp.sin(two_pi * along)[:, None, :]

    def incident(rows):
        real = across_cos[:, rows] * along_cos - across_sin[:, rows] * along_sin
        imag = across_sin[:, rows] * along_cos + across_cos[:, rows] * along_sin
        return real, imag

    halo = extended(screens[0], (("tile", 0),), HALF)
    pieces = [
        transmit(*incident(rows), screen)
        for rows, screen in (
            (slice(0, HALF), halo[:HALF]),
            (slice(HALF, HALF + local_rows), screens[0]),
            (slice(HALF + local_rows, span), halo[HALF + local_rows :]),
        )
    ]
    real = jnp.concatenate([piece[0] for piece in pieces], axis=1)
    imag = jnp.concatenate([piece[1] for piece in pieces], axis=1)
    real, imag = cross_pass(real, imag, taps)
    real, imag = along_pass(real, imag, taps)
    for plane in range(1, PLANES):
        real, imag = transmit(real, imag, screens[plane])
        packed = extended(jnp.stack([real, imag]), (("tile", 2),), HALF)
        real, imag = cross_pass(packed[0], packed[1], taps)
        real, imag = along_pass(real, imag, taps)
    return jnp.stack([real, imag])


def solution(mesh):
    in_specs = (P("illum", None), P(), P(None, "tile", "illum"), P())
    out_specs = P(None, "illum", "tile", None)
    return jax.shard_map(body, mesh=mesh, in_specs=in_specs, out_specs=out_specs, check_vma=False)
```

```python
import jax
import jax.numpy as jnp
from jax import lax
from jax.sharding import PartitionSpec as P

NY = 4096
PLANES = 2
HALF = 16


two_pi = 6.283185307179586


def extended(cells, sides, width):
    for axis, dim in sides:
        count = lax.axis_size(axis)
        ends = count - 1
        head = lax.slice_in_dim(cells, 0, width, axis=dim)
        tail = lax.slice_in_dim(cells, cells.shape[dim] - width, cells.shape[dim], axis=dim)
        cells = jnp.concatenate(
            [
                lax.ppermute(tail, axis, [(i, (i + 1) % count) for i in range(ends)]),
                cells,
                lax.ppermute(head, axis, [((i + 1) % count, i) for i in range(ends)]),
            ],
            axis=dim,
        )
    return cells


def toeplitz(tap_row, block):
    rows = jnp.arange(block + 2 * HALF)[:, None]
    cols = jnp.arange(block)[None, :]
    offset = rows - cols
    steps = jnp.arange(2 * HALF + 1)
    return jnp.sum(jnp.where(offset[:, :, None] == steps, tap_row, 0.0), axis=2)


def band_matrix(tap_row, count):
    rows = jnp.arange(count)[:, None]
    cols = jnp.arange(count + 2 * HALF)[None, :]
    offset = cols - rows
    steps = jnp.arange(2 * HALF + 1)
    return jnp.sum(jnp.where(offset[:, :, None] == steps, tap_row, 0.0), axis=2)


def windows(field, block):
    length = field.shape[-1]
    count = length // block
    widths = [(0, 0)] * (field.ndim - 1) + [(HALF, block - HALF)]
    padded = jnp.pad(field, widths)
    lead = field.shape[:-1]
    main = padded[..., :length].reshape(lead + (count, block))
    after = padded[..., block : length + block].reshape(lead + (count, block))[..., : 2 * HALF]
    return jnp.concatenate([main, after], axis=-1)


def complex_stack(real_part, imag_part):
    top = jnp.concatenate([real_part, -imag_part], axis=1)
    bottom = jnp.concatenate([imag_part, real_part], axis=1)
    return jnp.concatenate([top, bottom], axis=0)


def along_pass(real, imag, taps):
    block = min(128, real.shape[-1])
    win = jnp.concatenate([windows(real, block), windows(imag, block)], axis=-1)
    kern = complex_stack(toeplitz(taps[0], block), -toeplitz(taps[1], block))
    out = jnp.einsum("...nj,jc->...nc", win, kern, precision=lax.Precision.HIGH)
    return out[..., :block].reshape(real.shape), out[..., block:].reshape(real.shape)


def cross_pass(real, imag, taps):
    count = real.shape[1] - 2 * HALF
    band = complex_stack(band_matrix(taps[0], count), band_matrix(taps[1], count))
    field = jnp.concatenate([real, imag], axis=1)
    out = jnp.einsum("ij,ajy->aiy", band, field, precision=lax.Precision.HIGH)
    return out[:, :count], out[:, count:]


def transmit(real, imag, screen):
    cosine = jnp.cos(screen)
    sine = jnp.sin(screen)
    return (real * cosine - imag * sine, real * sine + imag * cosine)


def reorder(gathered, owner):
    count = gathered.shape[1]
    blocks = owner.shape[1]
    width = gathered.shape[2] // blocks
    planes = [
        gathered[p].reshape(count, blocks, width)[:, owner[p], :].reshape(count, blocks * width)
        for p in range(gathered.shape[0])
    ]
    return jnp.stack(planes)


def gather_screen(stored, order, axis):
    count = lax.axis_size(axis)
    me = lax.axis_index(axis)
    paired = count & (count - 1) == 0

    def partner(i, k):
        return i ^ k if paired else (i + k) % count

    parts = [stored]
    for k in range(1, count):
        parts.append(lax.ppermute(stored, axis, [(i, partner(i, k)) for i in range(count)]))
    stacked = jnp.stack(parts)
    source = jnp.bitwise_xor(me, order) if paired else jnp.mod(me - order, count)
    picked = stacked[source]
    return jnp.transpose(picked, (1, 0, 2)).reshape(stored.shape[0], count * stored.shape[1])


def body(tilts, taps, stored_planes, owner):
    local_rows = stored_planes.shape[1]
    total_rows = local_rows * lax.axis_size("tile")
    total_cols = NY
    first_row = lax.axis_index("tile") * local_rows
    screens = [gather_screen(stored_planes[0], owner[0], "illum")]
    extra = HALF
    span = local_rows + 2 * extra
    global_rows = first_row - extra + jnp.arange(span, dtype=jnp.int32)
    inside = (global_rows >= 0) & (global_rows < total_rows)
    cols = jnp.arange(total_cols, dtype=jnp.int32)
    across = (
        jnp.mod(tilts[:, 0:1] * global_rows[None, :], total_rows).astype(jnp.float32) / total_rows
    )
    along = jnp.mod(tilts[:, 1:2] * cols[None, :], total_cols).astype(jnp.float32) / total_cols
    across_cos = jnp.where(inside[None, :], jnp.cos(two_pi * across), 0.0)[:, :, None]
    across_sin = jnp.where(inside[None, :], jnp.sin(two_pi * across), 0.0)[:, :, None]
    along_cos = jnp.cos(two_pi * along)[:, None, :]
    along_sin = jnp.sin(two_pi * along)[:, None, :]

    def incident(rows):
        real = across_cos[:, rows] * along_cos - across_sin[:, rows] * along_sin
        imag = across_sin[:, rows] * along_cos + across_cos[:, rows] * along_sin
        return real, imag

    halo = extended(screens[0], (("tile", 0),), HALF)
    for plane in range(1, PLANES):
        ready = halo[0, 0] * 0.0 + halo[span - 1, 0] * 0.0
        screens.append(gather_screen(stored_planes[plane] + ready, owner[plane], "illum"))
    pieces = [
        transmit(*incident(rows), screen)
        for rows, screen in (
            (slice(0, HALF), halo[:HALF]),
            (slice(HALF, HALF + local_rows), screens[0]),
            (slice(HALF + local_rows, span), halo[HALF + local_rows :]),
        )
    ]
    real = jnp.concatenate([piece[0] for piece in pieces], axis=1)
    imag = jnp.concatenate([piece[1] for piece in pieces], axis=1)
    real, imag = cross_pass(real, imag, taps)
    real, imag = along_pass(real, imag, taps)
    for plane in range(1, PLANES):
        real, imag = transmit(real, imag, screens[plane])
        packed = extended(jnp.stack([real, imag]), (("tile", 2),), HALF)
        real, imag = cross_pass(packed[0], packed[1], taps)
        real, imag = along_pass(real, imag, taps)
    return jnp.stack([real, imag])


def solution(mesh):
    in_specs = (P("illum", None), P(), P(None, "tile", "illum"), P())
    out_specs = P(None, "illum", "tile", None)
    return jax.shard_map(body, mesh=mesh, in_specs=in_specs, out_specs=out_specs, check_vma=False)
```

```python
import jax
import jax.numpy as jnp
from jax import lax
from jax.sharding import PartitionSpec as P

NY = 4096
PLANES = 2
HALF = 16


two_pi = 6.283185307179586


def extended(cells, sides, width):
    for axis, dim in sides:
        count = lax.axis_size(axis)
        ends = count - 1
        head = lax.slice_in_dim(cells, 0, width, axis=dim)
        tail = lax.slice_in_dim(cells, cells.shape[dim] - width, cells.shape[dim], axis=dim)
        cells = jnp.concatenate(
            [
                lax.ppermute(tail, axis, [(i, (i + 1) % count) for i in range(ends)]),
                cells,
                lax.ppermute(head, axis, [((i + 1) % count, i) for i in range(ends)]),
            ],
            axis=dim,
        )
    return cells


def toeplitz(tap_row, block):
    rows = jnp.arange(block + 2 * HALF)[:, None]
    cols = jnp.arange(block)[None, :]
    offset = rows - cols
    steps = jnp.arange(2 * HALF + 1)
    return jnp.sum(jnp.where(offset[:, :, None] == steps, tap_row, 0.0), axis=2)


def band_matrix(tap_row, count):
    rows = jnp.arange(count)[:, None]
    cols = jnp.arange(count + 2 * HALF)[None, :]
    offset = cols - rows
    steps = jnp.arange(2 * HALF + 1)
    return jnp.sum(jnp.where(offset[:, :, None] == steps, tap_row, 0.0), axis=2)


def windows(field, block):
    length = field.shape[-1]
    count = length // block
    widths = [(0, 0)] * (field.ndim - 1) + [(HALF, block - HALF)]
    padded = jnp.pad(field, widths)
    lead = field.shape[:-1]
    main = padded[..., :length].reshape(lead + (count, block))
    after = padded[..., block : length + block].reshape(lead + (count, block))[..., : 2 * HALF]
    return jnp.concatenate([main, after], axis=-1)


def complex_stack(real_part, imag_part):
    top = jnp.concatenate([real_part, -imag_part], axis=1)
    bottom = jnp.concatenate([imag_part, real_part], axis=1)
    return jnp.concatenate([top, bottom], axis=0)


def along_pass(real, imag, taps):
    block = min(128, real.shape[-1])
    win = jnp.concatenate([windows(real, block), windows(imag, block)], axis=-1)
    kern = complex_stack(toeplitz(taps[0], block), -toeplitz(taps[1], block))
    out = jnp.einsum("...nj,jc->...nc", win, kern, precision=lax.Precision.HIGH)
    return out[..., :block].reshape(real.shape), out[..., block:].reshape(real.shape)


def cross_pass(real, imag, taps):
    count = real.shape[1] - 2 * HALF
    band = complex_stack(band_matrix(taps[0], count), band_matrix(taps[1], count))
    field = jnp.concatenate([real, imag], axis=1)
    out = jnp.einsum("ij,ajy->aiy", band, field, precision=lax.Precision.HIGH)
    return out[:, :count], out[:, count:]


def transmit(real, imag, screen):
    cosine = jnp.cos(screen)
    sine = jnp.sin(screen)
    return (real * cosine - imag * sine, real * sine + imag * cosine)


def reorder(gathered, owner):
    count = gathered.shape[1]
    blocks = owner.shape[1]
    width = gathered.shape[2] // blocks
    planes = [
        gathered[p].reshape(count, blocks, width)[:, owner[p], :].reshape(count, blocks * width)
        for p in range(gathered.shape[0])
    ]
    return jnp.stack(planes)


def gather_screens(stored_planes, owner, axis):
    count = lax.axis_size(axis)
    me = lax.axis_index(axis)
    paired = count & (count - 1) == 0

    def partner(i, k):
        return i ^ k if paired else (i + k) % count

    parts = [stored_planes]
    for k in range(1, count):
        parts.append(lax.ppermute(stored_planes, axis, [(i, partner(i, k)) for i in range(count)]))
    stacked = jnp.stack(parts, axis=1)
    rows = stored_planes.shape[1]
    width = stored_planes.shape[2]
    planes = []
    for p in range(stored_planes.shape[0]):
        source = jnp.bitwise_xor(me, owner[p]) if paired else jnp.mod(me - owner[p], count)
        picked = stacked[p][source]
        planes.append(jnp.transpose(picked, (1, 0, 2)).reshape(rows, count * width))
    return jnp.stack(planes)


def around(arrays, reaches, axis):
    count = lax.axis_size(axis)
    local = arrays[0].shape[0]
    below = [[] for _ in arrays]
    above = [[] for _ in arrays]
    for distance in range(1, max(-(-r // local) for r in reaches) + 1):
        for down in (True, False):
            spans = []
            for x, reach in zip(arrays, reaches):
                if down:
                    lo, hi = max(distance * local - reach, 0), local
                else:
                    lo, hi = 0, min(local, reach - (distance - 1) * local)
                spans.append((lo, hi) if hi > lo else None)
            taken = [x[lo:hi] for x, span in zip(arrays, spans) if span for lo, hi in [span]]
            if not taken:
                continue
            if down:
                pairs = [(i, i + distance) for i in range(count - distance)]
            else:
                pairs = [(i + distance, i) for i in range(count - distance)]
            got = lax.ppermute(jnp.concatenate(taken, axis=0), axis, pairs)
            at = 0
            for k, span in enumerate(spans):
                if span:
                    piece = got[at : at + span[1] - span[0]]
                    at += span[1] - span[0]
                    if down:
                        below[k].insert(0, piece)
                    else:
                        above[k].append(piece)
    return [(b, x, a) for b, x, a in zip(below, arrays, above)]


def body(tilts, taps, stored_planes, owner):
    local_rows = stored_planes.shape[1]
    total_rows = local_rows * lax.axis_size("tile")
    total_cols = NY
    first_row = lax.axis_index("tile") * local_rows
    screens = gather_screens(stored_planes, owner, "illum")
    reaches = [(PLANES - plane) * HALF for plane in range(PLANES)]
    extended_screens = around([screens[plane] for plane in range(PLANES)], reaches, "tile")
    cols = jnp.arange(total_cols, dtype=jnp.int32)
    along = jnp.mod(tilts[:, 1:2] * cols[None, :], total_cols).astype(jnp.float32) / total_cols
    along_cos = jnp.cos(two_pi * along)[:, None, :]
    along_sin = jnp.sin(two_pi * along)[:, None, :]

    def rows_from(start, count):
        global_rows = first_row + start + jnp.arange(count, dtype=jnp.int32)
        return global_rows, (global_rows >= 0) & (global_rows < total_rows)

    def incident(start, count):
        global_rows, inside = rows_from(start, count)
        across = jnp.mod(tilts[:, 0:1] * global_rows[None, :], total_rows).astype(jnp.float32) / total_rows
        across_cos = jnp.where(inside[None, :], jnp.cos(two_pi * across), 0.0)[:, :, None]
        across_sin = jnp.where(inside[None, :], jnp.sin(two_pi * across), 0.0)[:, :, None]
        real = across_cos * along_cos - across_sin * along_sin
        imag = across_sin * along_cos + across_cos * along_sin
        return real, imag

    reach = reaches[0]
    pieces = []
    start = -reach
    for group in extended_screens[0]:
        for screen in group if isinstance(group, list) else [group]:
            pieces.append(transmit(*incident(start, screen.shape[0]), screen))
            start += screen.shape[0]
    real = jnp.concatenate([piece[0] for piece in pieces], axis=1)
    imag = jnp.concatenate([piece[1] for piece in pieces], axis=1)
    for plane in range(PLANES):
        real, imag = cross_pass(real, imag, taps)
        real, imag = along_pass(real, imag, taps)
        if plane + 1 < PLANES:
            reach = reaches[plane + 1]
            _, inside = rows_from(-reach, local_rows + 2 * reach)
            below, own, above = extended_screens[plane + 1]
            screen = jnp.concatenate(below + [own] + above, axis=0)
            real = jnp.where(inside[None, :, None], real, 0.0)
            imag = jnp.where(inside[None, :, None], imag, 0.0)
            real, imag = transmit(real, imag, screen)
    return jnp.stack([real, imag])


def solution(mesh):
    in_specs = (P("illum", None), P(), P(None, "tile", "illum"), P())
    out_specs = P(None, "illum", "tile", None)
    return jax.shard_map(body, mesh=mesh, in_specs=in_specs, out_specs=out_specs, check_vma=False)
```

```python
import jax
import jax.numpy as jnp
from jax import lax
from jax.sharding import PartitionSpec as P

NY = 4096
PLANES = 2
HALF = 16


two_pi = 6.283185307179586


def extended(cells, sides, width):
    for axis, dim in sides:
        count = lax.axis_size(axis)
        ends = count - 1
        head = lax.slice_in_dim(cells, 0, width, axis=dim)
        tail = lax.slice_in_dim(cells, cells.shape[dim] - width, cells.shape[dim], axis=dim)
        cells = jnp.concatenate(
            [
                lax.ppermute(tail, axis, [(i, (i + 1) % count) for i in range(ends)]),
                cells,
                lax.ppermute(head, axis, [((i + 1) % count, i) for i in range(ends)]),
            ],
            axis=dim,
        )
    return cells


def toeplitz(tap_row, block):
    rows = jnp.arange(block + 2 * HALF)[:, None]
    cols = jnp.arange(block)[None, :]
    offset = rows - cols
    steps = jnp.arange(2 * HALF + 1)
    return jnp.sum(jnp.where(offset[:, :, None] == steps, tap_row, 0.0), axis=2)


def band_matrix(tap_row, count):
    rows = jnp.arange(count)[:, None]
    cols = jnp.arange(count + 2 * HALF)[None, :]
    offset = cols - rows
    steps = jnp.arange(2 * HALF + 1)
    return jnp.sum(jnp.where(offset[:, :, None] == steps, tap_row, 0.0), axis=2)


def windows(field, block):
    length = field.shape[-1]
    count = length // block
    widths = [(0, 0)] * (field.ndim - 1) + [(HALF, block - HALF)]
    padded = jnp.pad(field, widths)
    lead = field.shape[:-1]
    main = padded[..., :length].reshape(lead + (count, block))
    after = padded[..., block : length + block].reshape(lead + (count, block))[..., : 2 * HALF]
    return jnp.concatenate([main, after], axis=-1)


def complex_stack(real_part, imag_part):
    top = jnp.concatenate([real_part, -imag_part], axis=1)
    bottom = jnp.concatenate([imag_part, real_part], axis=1)
    return jnp.concatenate([top, bottom], axis=0)


def along_pass(real, imag, taps):
    block = min(128, real.shape[-1])
    win = jnp.concatenate([windows(real, block), windows(imag, block)], axis=-1)
    kern = complex_stack(toeplitz(taps[0], block), -toeplitz(taps[1], block))
    out = jnp.einsum("...nj,jc->...nc", win, kern, precision=lax.Precision.HIGH)
    return out[..., :block].reshape(real.shape), out[..., block:].reshape(real.shape)


def cross_pass(real, imag, taps):
    count = real.shape[1] - 2 * HALF
    band = complex_stack(band_matrix(taps[0], count), band_matrix(taps[1], count))
    field = jnp.concatenate([real, imag], axis=1)
    out = jnp.einsum("ij,ajy->aiy", band, field, precision=lax.Precision.HIGH)
    return out[:, :count], out[:, count:]


def transmit(real, imag, screen):
    cosine = jnp.cos(screen)
    sine = jnp.sin(screen)
    return (real * cosine - imag * sine, real * sine + imag * cosine)


def reorder(gathered, owner):
    count = gathered.shape[1]
    blocks = owner.shape[1]
    width = gathered.shape[2] // blocks
    planes = [
        gathered[p].reshape(count, blocks, width)[:, owner[p], :].reshape(count, blocks * width)
        for p in range(gathered.shape[0])
    ]
    return jnp.stack(planes)


def gather_screens(stored_planes, owner, axis):
    count = lax.axis_size(axis)
    me = lax.axis_index(axis)
    paired = count & (count - 1) == 0

    def partner(i, k):
        return i ^ k if paired else (i + k) % count

    def exchange(x, k):
        return lax.ppermute(x, axis, [(i, partner(i, k)) for i in range(count)])

    if count == 8:
        one, two, four = (exchange(stored_planes, k) for k in (1, 2, 4))
        three, five = exchange(jnp.stack([two, four]), 1)
        six = exchange(four, 2)
        seven = exchange(one, 6)
        parts = [stored_planes, one, two, three, four, five, six, seven]
    else:
        parts = [stored_planes] + [exchange(stored_planes, k) for k in range(1, count)]
    stacked = jnp.stack(parts, axis=1)
    rows = stored_planes.shape[1]
    width = stored_planes.shape[2]
    planes = []
    for p in range(stored_planes.shape[0]):
        source = jnp.bitwise_xor(me, owner[p]) if paired else jnp.mod(me - owner[p], count)
        picked = stacked[p][source]
        planes.append(jnp.transpose(picked, (1, 0, 2)).reshape(rows, count * width))
    return jnp.stack(planes)


def body(tilts, taps, stored_planes, owner):
    local_rows = stored_planes.shape[1]
    total_rows = local_rows * lax.axis_size("tile")
    total_cols = NY
    first_row = lax.axis_index("tile") * local_rows
    screens = gather_screens(stored_planes, owner, "illum")
    extra = HALF
    span = local_rows + 2 * extra
    global_rows = first_row - extra + jnp.arange(span, dtype=jnp.int32)
    inside = (global_rows >= 0) & (global_rows < total_rows)
    cols = jnp.arange(total_cols, dtype=jnp.int32)
    across = (
        jnp.mod(tilts[:, 0:1] * global_rows[None, :], total_rows).astype(jnp.float32) / total_rows
    )
    along = jnp.mod(tilts[:, 1:2] * cols[None, :], total_cols).astype(jnp.float32) / total_cols
    across_cos = jnp.where(inside[None, :], jnp.cos(two_pi * across), 0.0)[:, :, None]
    across_sin = jnp.where(inside[None, :], jnp.sin(two_pi * across), 0.0)[:, :, None]
    along_cos = jnp.cos(two_pi * along)[:, None, :]
    along_sin = jnp.sin(two_pi * along)[:, None, :]

    def incident(rows):
        real = across_cos[:, rows] * along_cos - across_sin[:, rows] * along_sin
        imag = across_sin[:, rows] * along_cos + across_cos[:, rows] * along_sin
        return real, imag

    halo = extended(screens[0], (("tile", 0),), HALF)
    pieces = [
        transmit(*incident(rows), screen)
        for rows, screen in (
            (slice(0, HALF), halo[:HALF]),
            (slice(HALF, HALF + local_rows), screens[0]),
            (slice(HALF + local_rows, span), halo[HALF + local_rows :]),
        )
    ]
    real = jnp.concatenate([piece[0] for piece in pieces], axis=1)
    imag = jnp.concatenate([piece[1] for piece in pieces], axis=1)
    real, imag = cross_pass(real, imag, taps)
    real, imag = along_pass(real, imag, taps)
    for plane in range(1, PLANES):
        real, imag = transmit(real, imag, screens[plane])
        packed = extended(jnp.stack([real, imag]), (("tile", 2),), HALF)
        real, imag = cross_pass(packed[0], packed[1], taps)
        real, imag = along_pass(real, imag, taps)
    return jnp.stack([real, imag])


def solution(mesh):
    in_specs = (P("illum", None), P(), P(None, "tile", "illum"), P())
    out_specs = P(None, "illum", "tile", None)
    return jax.shard_map(body, mesh=mesh, in_specs=in_specs, out_specs=out_specs, check_vma=False)
```

```python
import jax
import jax.numpy as jnp
from jax import lax
from jax.sharding import PartitionSpec as P

NY = 4096
PLANES = 2
HALF = 16


two_pi = 6.283185307179586


def extended(cells, sides, width):
    for axis, dim in sides:
        count = lax.axis_size(axis)
        ends = count - 1
        head = lax.slice_in_dim(cells, 0, width, axis=dim)
        tail = lax.slice_in_dim(cells, cells.shape[dim] - width, cells.shape[dim], axis=dim)
        cells = jnp.concatenate(
            [
                lax.ppermute(tail, axis, [(i, (i + 1) % count) for i in range(ends)]),
                cells,
                lax.ppermute(head, axis, [((i + 1) % count, i) for i in range(ends)]),
            ],
            axis=dim,
        )
    return cells


def toeplitz(tap_row, block):
    rows = jnp.arange(block + 2 * HALF)[:, None]
    cols = jnp.arange(block)[None, :]
    offset = rows - cols
    steps = jnp.arange(2 * HALF + 1)
    return jnp.sum(jnp.where(offset[:, :, None] == steps, tap_row, 0.0), axis=2)


def band_matrix(tap_row, count):
    rows = jnp.arange(count)[:, None]
    cols = jnp.arange(count + 2 * HALF)[None, :]
    offset = cols - rows
    steps = jnp.arange(2 * HALF + 1)
    return jnp.sum(jnp.where(offset[:, :, None] == steps, tap_row, 0.0), axis=2)


def windows(field, block):
    length = field.shape[-1]
    count = length // block
    widths = [(0, 0)] * (field.ndim - 1) + [(HALF, block - HALF)]
    padded = jnp.pad(field, widths)
    lead = field.shape[:-1]
    main = padded[..., :length].reshape(lead + (count, block))
    after = padded[..., block : length + block].reshape(lead + (count, block))[..., : 2 * HALF]
    return jnp.concatenate([main, after], axis=-1)


def complex_stack(real_part, imag_part):
    top = jnp.concatenate([real_part, -imag_part], axis=1)
    bottom = jnp.concatenate([imag_part, real_part], axis=1)
    return jnp.concatenate([top, bottom], axis=0)


def along_pass(real, imag, taps):
    block = min(128, real.shape[-1])
    win = jnp.concatenate([windows(real, block), windows(imag, block)], axis=-1)
    kern = complex_stack(toeplitz(taps[0], block), -toeplitz(taps[1], block))
    out = jnp.einsum("...nj,jc->...nc", win, kern, precision=lax.Precision.HIGH)
    return out[..., :block].reshape(real.shape), out[..., block:].reshape(real.shape)


def cross_pass(real, imag, taps):
    count = real.shape[1] - 2 * HALF
    band = complex_stack(band_matrix(taps[0], count), band_matrix(taps[1], count))
    field = jnp.concatenate([real, imag], axis=1)
    out = jnp.einsum("ij,ajy->aiy", band, field, precision=lax.Precision.HIGH)
    return out[:, :count], out[:, count:]


def transmit(real, imag, screen):
    cosine = jnp.cos(screen)
    sine = jnp.sin(screen)
    return (real * cosine - imag * sine, real * sine + imag * cosine)


def reorder(gathered, owner):
    count = gathered.shape[1]
    blocks = owner.shape[1]
    width = gathered.shape[2] // blocks
    planes = [
        gathered[p].reshape(count, blocks, width)[:, owner[p], :].reshape(count, blocks * width)
        for p in range(gathered.shape[0])
    ]
    return jnp.stack(planes)


def gather_screens(stored_planes, selections, axis):
    count = lax.axis_size(axis)
    me = lax.axis_index(axis)
    paired = count & (count - 1) == 0

    def partner(i, k):
        return i ^ k if paired else (i + k) % count

    def exchange(x, k):
        return lax.ppermute(x, axis, [(i, partner(i, k)) for i in range(count)])

    if count == 8:
        one, two, four = (exchange(stored_planes, k) for k in (1, 2, 4))
        three, five = exchange(jnp.stack([two, four]), 1)
        six = exchange(four, 2)
        seven = exchange(one, 6)
        parts = [stored_planes, one, two, three, four, five, six, seven]
    else:
        parts = [stored_planes] + [exchange(stored_planes, k) for k in range(1, count)]
    stacked = jnp.stack(parts)
    width = stored_planes.shape[1]
    screens = []
    for lo, hi, order in selections:
        source = jnp.bitwise_xor(me, order) if paired else jnp.mod(me - order, count)
        picked = stacked[:, lo:hi][source]
        screens.append(jnp.transpose(picked, (1, 0, 2)).reshape(hi - lo, count * width))
    return screens


def body(tilts, taps, stored_planes, owner):
    local_rows = stored_planes.shape[1]
    total_rows = local_rows * lax.axis_size("tile")
    total_cols = NY
    first_row = lax.axis_index("tile") * local_rows
    extra = HALF
    first_block = extended(stored_planes[0], (("tile", 0),), HALF)
    block = jnp.concatenate([first_block] + [stored_planes[plane] for plane in range(1, PLANES)], axis=0)
    selections = [(0, local_rows + 2 * extra, owner[0])]
    for plane in range(1, PLANES):
        lo = local_rows + 2 * extra + (plane - 1) * local_rows
        selections.append((lo, lo + local_rows, owner[plane]))
    screens = gather_screens(block, selections, "illum")
    span = local_rows + 2 * extra
    global_rows = first_row - extra + jnp.arange(span, dtype=jnp.int32)
    inside = (global_rows >= 0) & (global_rows < total_rows)
    cols = jnp.arange(total_cols, dtype=jnp.int32)
    across = (
        jnp.mod(tilts[:, 0:1] * global_rows[None, :], total_rows).astype(jnp.float32) / total_rows
    )
    along = jnp.mod(tilts[:, 1:2] * cols[None, :], total_cols).astype(jnp.float32) / total_cols
    across_cos = jnp.where(inside[None, :], jnp.cos(two_pi * across), 0.0)[:, :, None]
    across_sin = jnp.where(inside[None, :], jnp.sin(two_pi * across), 0.0)[:, :, None]
    along_cos = jnp.cos(two_pi * along)[:, None, :]
    along_sin = jnp.sin(two_pi * along)[:, None, :]

    def incident(rows):
        real = across_cos[:, rows] * along_cos - across_sin[:, rows] * along_sin
        imag = across_sin[:, rows] * along_cos + across_cos[:, rows] * along_sin
        return real, imag

    real, imag = transmit(*incident(slice(0, span)), screens[0])
    real, imag = cross_pass(real, imag, taps)
    real, imag = along_pass(real, imag, taps)
    for plane in range(1, PLANES):
        real, imag = transmit(real, imag, screens[plane])
        packed = extended(jnp.stack([real, imag]), (("tile", 2),), HALF)
        real, imag = cross_pass(packed[0], packed[1], taps)
        real, imag = along_pass(real, imag, taps)
    return jnp.stack([real, imag])


def solution(mesh):
    in_specs = (P("illum", None), P(), P(None, "tile", "illum"), P())
    out_specs = P(None, "illum", "tile", None)
    return jax.shard_map(body, mesh=mesh, in_specs=in_specs, out_specs=out_specs, check_vma=False)
```

```python
import jax
import jax.numpy as jnp
from jax import lax
from jax.sharding import PartitionSpec as P

NY = 4096
PLANES = 2
HALF = 16


two_pi = 6.283185307179586


def extended(cells, sides, width):
    for axis, dim in sides:
        count = lax.axis_size(axis)
        ends = count - 1
        head = lax.slice_in_dim(cells, 0, width, axis=dim)
        tail = lax.slice_in_dim(cells, cells.shape[dim] - width, cells.shape[dim], axis=dim)
        cells = jnp.concatenate(
            [
                lax.ppermute(tail, axis, [(i, (i + 1) % count) for i in range(ends)]),
                cells,
                lax.ppermute(head, axis, [((i + 1) % count, i) for i in range(ends)]),
            ],
            axis=dim,
        )
    return cells


def toeplitz(tap_row, block):
    rows = jnp.arange(block + 2 * HALF)[:, None]
    cols = jnp.arange(block)[None, :]
    offset = rows - cols
    steps = jnp.arange(2 * HALF + 1)
    return jnp.sum(jnp.where(offset[:, :, None] == steps, tap_row, 0.0), axis=2)


def band_matrix(tap_row, count):
    rows = jnp.arange(count)[:, None]
    cols = jnp.arange(count + 2 * HALF)[None, :]
    offset = cols - rows
    steps = jnp.arange(2 * HALF + 1)
    return jnp.sum(jnp.where(offset[:, :, None] == steps, tap_row, 0.0), axis=2)


def windows(field, block):
    length = field.shape[-1]
    count = length // block
    widths = [(0, 0)] * (field.ndim - 1) + [(HALF, block - HALF)]
    padded = jnp.pad(field, widths)
    lead = field.shape[:-1]
    main = padded[..., :length].reshape(lead + (count, block))
    after = padded[..., block : length + block].reshape(lead + (count, block))[..., : 2 * HALF]
    return jnp.concatenate([main, after], axis=-1)


def complex_stack(real_part, imag_part):
    top = jnp.concatenate([real_part, -imag_part], axis=1)
    bottom = jnp.concatenate([imag_part, real_part], axis=1)
    return jnp.concatenate([top, bottom], axis=0)


def along_pass(real, imag, taps):
    block = min(128, real.shape[-1])
    win = jnp.concatenate([windows(real, block), windows(imag, block)], axis=-1)
    kern = complex_stack(toeplitz(taps[0], block), -toeplitz(taps[1], block))
    out = jnp.einsum("...nj,jc->...nc", win, kern, precision=lax.Precision.HIGH)
    return out[..., :block].reshape(real.shape), out[..., block:].reshape(real.shape)


def cross_pass(real, imag, taps):
    count = real.shape[1] - 2 * HALF
    band = complex_stack(band_matrix(taps[0], count), band_matrix(taps[1], count))
    field = jnp.concatenate([real, imag], axis=1)
    out = jnp.einsum("ij,ajy->aiy", band, field, precision=lax.Precision.HIGH)
    return out[:, :count], out[:, count:]


def transmit(real, imag, screen):
    cosine = jnp.cos(screen)
    sine = jnp.sin(screen)
    return (real * cosine - imag * sine, real * sine + imag * cosine)


def reorder(gathered, owner):
    count = gathered.shape[1]
    blocks = owner.shape[1]
    width = gathered.shape[2] // blocks
    planes = [
        gathered[p].reshape(count, blocks, width)[:, owner[p], :].reshape(count, blocks * width)
        for p in range(gathered.shape[0])
    ]
    return jnp.stack(planes)


def gather_screens(stored_planes, owner, axis):
    count = lax.axis_size(axis)
    me = lax.axis_index(axis)
    paired = count & (count - 1) == 0

    def partner(i, k):
        return i ^ k if paired else (i + k) % count

    def exchange(x, k):
        return lax.ppermute(x, axis, [(i, partner(i, k)) for i in range(count)])

    if count == 8:
        one, two, four = (exchange(stored_planes, k) for k in (1, 2, 4))
        three, five = exchange(jnp.stack([two, four]), 1)
        six = exchange(four, 2)
        seven = exchange(one, 6)
        parts = [stored_planes, one, two, three, four, five, six, seven]
        first = [three, six, seven]
    else:
        parts = [stored_planes] + [exchange(stored_planes, k) for k in range(1, count)]
        first = parts[1:]
    landed = sum(part[0, 0, 0] for part in first) * 0.0
    stacked = jnp.stack(parts, axis=1)
    rows = stored_planes.shape[1]
    width = stored_planes.shape[2]
    planes = []
    for p in range(stored_planes.shape[0]):
        source = jnp.bitwise_xor(me, owner[p]) if paired else jnp.mod(me - owner[p], count)
        picked = stacked[p][source]
        planes.append(jnp.transpose(picked, (1, 0, 2)).reshape(rows, count * width))
    return jnp.stack(planes), landed


def body(tilts, taps, stored_planes, owner):
    local_rows = stored_planes.shape[1]
    total_rows = local_rows * lax.axis_size("tile")
    total_cols = NY
    first_row = lax.axis_index("tile") * local_rows
    screens, landed = gather_screens(stored_planes, owner, "illum")
    taps = taps + landed
    extra = HALF
    span = local_rows + 2 * extra
    global_rows = first_row - extra + jnp.arange(span, dtype=jnp.int32)
    inside = (global_rows >= 0) & (global_rows < total_rows)
    cols = jnp.arange(total_cols, dtype=jnp.int32)
    across = (
        jnp.mod(tilts[:, 0:1] * global_rows[None, :], total_rows).astype(jnp.float32) / total_rows
    )
    along = jnp.mod(tilts[:, 1:2] * cols[None, :], total_cols).astype(jnp.float32) / total_cols
    across_cos = jnp.where(inside[None, :], jnp.cos(two_pi * across), 0.0)[:, :, None]
    across_sin = jnp.where(inside[None, :], jnp.sin(two_pi * across), 0.0)[:, :, None]
    along_cos = jnp.cos(two_pi * along)[:, None, :]
    along_sin = jnp.sin(two_pi * along)[:, None, :]

    def incident(rows):
        real = across_cos[:, rows] * along_cos - across_sin[:, rows] * along_sin
        imag = across_sin[:, rows] * along_cos + across_cos[:, rows] * along_sin
        return real, imag

    halo = extended(screens[0], (("tile", 0),), HALF)
    pieces = [
        transmit(*incident(rows), screen)
        for rows, screen in (
            (slice(0, HALF), halo[:HALF]),
            (slice(HALF, HALF + local_rows), screens[0]),
            (slice(HALF + local_rows, span), halo[HALF + local_rows :]),
        )
    ]
    real = jnp.concatenate([piece[0] for piece in pieces], axis=1)
    imag = jnp.concatenate([piece[1] for piece in pieces], axis=1)
    real, imag = cross_pass(real, imag, taps)
    real, imag = along_pass(real, imag, taps)
    for plane in range(1, PLANES):
        real, imag = transmit(real, imag, screens[plane])
        packed = extended(jnp.stack([real, imag]), (("tile", 2),), HALF)
        real, imag = cross_pass(packed[0], packed[1], taps)
        real, imag = along_pass(real, imag, taps)
    return jnp.stack([real, imag])


def solution(mesh):
    in_specs = (P("illum", None), P(), P(None, "tile", "illum"), P())
    out_specs = P(None, "illum", "tile", None)
    return jax.shard_map(body, mesh=mesh, in_specs=in_specs, out_specs=out_specs, check_vma=False)
```

```python
import jax
import jax.numpy as jnp
from jax import lax
from jax.sharding import PartitionSpec as P

NY = 4096
PLANES = 2
HALF = 16


two_pi = 6.283185307179586


def extended(cells, sides, width):
    for axis, dim in sides:
        count = lax.axis_size(axis)
        ends = count - 1
        head = lax.slice_in_dim(cells, 0, width, axis=dim)
        tail = lax.slice_in_dim(cells, cells.shape[dim] - width, cells.shape[dim], axis=dim)
        cells = jnp.concatenate(
            [
                lax.ppermute(tail, axis, [(i, (i + 1) % count) for i in range(ends)]),
                cells,
                lax.ppermute(head, axis, [((i + 1) % count, i) for i in range(ends)]),
            ],
            axis=dim,
        )
    return cells


def toeplitz(tap_row, block):
    rows = jnp.arange(block + 2 * HALF)[:, None]
    cols = jnp.arange(block)[None, :]
    offset = rows - cols
    steps = jnp.arange(2 * HALF + 1)
    return jnp.sum(jnp.where(offset[:, :, None] == steps, tap_row, 0.0), axis=2)


def band_matrix(tap_row, count):
    rows = jnp.arange(count)[:, None]
    cols = jnp.arange(count + 2 * HALF)[None, :]
    offset = cols - rows
    steps = jnp.arange(2 * HALF + 1)
    return jnp.sum(jnp.where(offset[:, :, None] == steps, tap_row, 0.0), axis=2)


def windows(field, block):
    length = field.shape[-1]
    count = length // block
    widths = [(0, 0)] * (field.ndim - 1) + [(HALF, block - HALF)]
    padded = jnp.pad(field, widths)
    lead = field.shape[:-1]
    main = padded[..., :length].reshape(lead + (count, block))
    after = padded[..., block : length + block].reshape(lead + (count, block))[..., : 2 * HALF]
    return jnp.concatenate([main, after], axis=-1)


def complex_stack(real_part, imag_part):
    top = jnp.concatenate([real_part, -imag_part], axis=1)
    bottom = jnp.concatenate([imag_part, real_part], axis=1)
    return jnp.concatenate([top, bottom], axis=0)


def along_pass(packed, taps):
    block = min(128, packed.shape[-1])
    win = windows(packed, block)
    kern = complex_stack(toeplitz(taps[0], block), -toeplitz(taps[1], block))
    kern = kern.reshape(2, block + 2 * HALF, 2, block)
    out = jnp.einsum("q...nj,qjpc->p...nc", win, kern, precision=lax.Precision.HIGH)
    return out.reshape(packed.shape)


def cross_pass(packed, taps):
    count = packed.shape[-2] - 2 * HALF
    band = complex_stack(band_matrix(taps[0], count), band_matrix(taps[1], count))
    band = band.reshape(2, count, 2, count + 2 * HALF)
    return jnp.einsum("piqj,q...jy->p...iy", band, packed, precision=lax.Precision.HIGH)


def transmit(real, imag, screen):
    cosine = jnp.cos(screen)
    sine = jnp.sin(screen)
    return (real * cosine - imag * sine, real * sine + imag * cosine)


def reorder(gathered, owner):
    count = gathered.shape[1]
    blocks = owner.shape[1]
    width = gathered.shape[2] // blocks
    planes = [
        gathered[p].reshape(count, blocks, width)[:, owner[p], :].reshape(count, blocks * width)
        for p in range(gathered.shape[0])
    ]
    return jnp.stack(planes)


def gather_screens(stored_planes, owner, axis):
    count = lax.axis_size(axis)
    me = lax.axis_index(axis)
    paired = count & (count - 1) == 0

    def partner(i, k):
        return i ^ k if paired else (i + k) % count

    def exchange(x, k):
        return lax.ppermute(x, axis, [(i, partner(i, k)) for i in range(count)])

    if count == 8:
        one, two, four = (exchange(stored_planes, k) for k in (1, 2, 4))
        three, five = exchange(jnp.stack([two, four]), 1)
        six = exchange(four, 2)
        seven = exchange(one, 6)
        parts = [stored_planes, one, two, three, four, five, six, seven]
        first = [three, six, seven]
    else:
        parts = [stored_planes] + [exchange(stored_planes, k) for k in range(1, count)]
        first = parts[1:]
    landed = sum(part[0, 0, 0] for part in first) * 0.0
    stacked = jnp.stack(parts, axis=1)
    rows = stored_planes.shape[1]
    width = stored_planes.shape[2]
    planes = []
    for p in range(stored_planes.shape[0]):
        source = jnp.bitwise_xor(me, owner[p]) if paired else jnp.mod(me - owner[p], count)
        picked = stacked[p][source]
        planes.append(jnp.transpose(picked, (1, 0, 2)).reshape(rows, count * width))
    return jnp.stack(planes), landed


def body(tilts, taps, stored_planes, owner):
    local_rows = stored_planes.shape[1]
    total_rows = local_rows * lax.axis_size("tile")
    total_cols = NY
    first_row = lax.axis_index("tile") * local_rows
    screens, landed = gather_screens(stored_planes, owner, "illum")
    taps = taps + landed
    extra = HALF
    span = local_rows + 2 * extra
    global_rows = first_row - extra + jnp.arange(span, dtype=jnp.int32)
    inside = (global_rows >= 0) & (global_rows < total_rows)
    cols = jnp.arange(total_cols, dtype=jnp.int32)
    across = (
        jnp.mod(tilts[:, 0:1] * global_rows[None, :], total_rows).astype(jnp.float32) / total_rows
    )
    along = jnp.mod(tilts[:, 1:2] * cols[None, :], total_cols).astype(jnp.float32) / total_cols
    across_cos = jnp.where(inside[None, :], jnp.cos(two_pi * across), 0.0)[:, :, None]
    across_sin = jnp.where(inside[None, :], jnp.sin(two_pi * across), 0.0)[:, :, None]
    along_cos = jnp.cos(two_pi * along)[:, None, :]
    along_sin = jnp.sin(two_pi * along)[:, None, :]

    def incident(rows):
        real = across_cos[:, rows] * along_cos - across_sin[:, rows] * along_sin
        imag = across_sin[:, rows] * along_cos + across_cos[:, rows] * along_sin
        return real, imag

    halo = extended(screens[0], (("tile", 0),), HALF)
    pieces = [
        transmit(*incident(rows), screen)
        for rows, screen in (
            (slice(0, HALF), halo[:HALF]),
            (slice(HALF, HALF + local_rows), screens[0]),
            (slice(HALF + local_rows, span), halo[HALF + local_rows :]),
        )
    ]
    real = jnp.concatenate([piece[0] for piece in pieces], axis=1)
    imag = jnp.concatenate([piece[1] for piece in pieces], axis=1)
    packed = along_pass(cross_pass(jnp.stack([real, imag]), taps), taps)
    for plane in range(1, PLANES):
        real, imag = transmit(packed[0], packed[1], screens[plane])
        packed = extended(jnp.stack([real, imag]), (("tile", 2),), HALF)
        packed = along_pass(cross_pass(packed, taps), taps)
    return packed


def solution(mesh):
    in_specs = (P("illum", None), P(), P(None, "tile", "illum"), P())
    out_specs = P(None, "illum", "tile", None)
    return jax.shard_map(body, mesh=mesh, in_specs=in_specs, out_specs=out_specs, check_vma=False)
```

```python
import jax
import jax.numpy as jnp
from jax import lax
from jax.sharding import PartitionSpec as P

NY = 4096
PLANES = 2
HALF = 16


two_pi = 6.283185307179586


def extended(cells, sides, width):
    for axis, dim in sides:
        count = lax.axis_size(axis)
        ends = count - 1
        head = lax.slice_in_dim(cells, 0, width, axis=dim)
        tail = lax.slice_in_dim(cells, cells.shape[dim] - width, cells.shape[dim], axis=dim)
        cells = jnp.concatenate(
            [
                lax.ppermute(tail, axis, [(i, (i + 1) % count) for i in range(ends)]),
                cells,
                lax.ppermute(head, axis, [((i + 1) % count, i) for i in range(ends)]),
            ],
            axis=dim,
        )
    return cells


def toeplitz(tap_row, block):
    rows = jnp.arange(block + 2 * HALF)[:, None]
    cols = jnp.arange(block)[None, :]
    offset = rows - cols
    steps = jnp.arange(2 * HALF + 1)
    return jnp.sum(jnp.where(offset[:, :, None] == steps, tap_row, 0.0), axis=2)


def band_matrix(tap_row, count):
    rows = jnp.arange(count)[:, None]
    cols = jnp.arange(count + 2 * HALF)[None, :]
    offset = cols - rows
    steps = jnp.arange(2 * HALF + 1)
    return jnp.sum(jnp.where(offset[:, :, None] == steps, tap_row, 0.0), axis=2)


def windows(field, block):
    length = field.shape[-1]
    count = length // block
    widths = [(0, 0)] * (field.ndim - 1) + [(HALF, block - HALF)]
    padded = jnp.pad(field, widths)
    lead = field.shape[:-1]
    main = padded[..., :length].reshape(lead + (count, block))
    after = padded[..., block : length + block].reshape(lead + (count, block))[..., : 2 * HALF]
    return jnp.concatenate([main, after], axis=-1)


def complex_stack(real_part, imag_part):
    top = jnp.concatenate([real_part, -imag_part], axis=1)
    bottom = jnp.concatenate([imag_part, real_part], axis=1)
    return jnp.concatenate([top, bottom], axis=0)


def along_pass(real, imag, taps):
    block = min(128, real.shape[-1])
    win = jnp.concatenate([windows(real, block), windows(imag, block)], axis=-1)
    kern = complex_stack(toeplitz(taps[0], block), -toeplitz(taps[1], block))
    out = jnp.einsum("...nj,jc->...nc", win, kern, precision=lax.Precision.HIGH)
    return out[..., :block].reshape(real.shape), out[..., block:].reshape(real.shape)


def cross_pass(real, imag, taps):
    count = real.shape[1] - 2 * HALF
    band = complex_stack(band_matrix(taps[0], count), band_matrix(taps[1], count))
    field = jnp.concatenate([real, imag], axis=1)
    out = jnp.einsum("ij,ajy->aiy", band, field, precision=lax.Precision.HIGH)
    return out[:, :count], out[:, count:]


def transmit(real, imag, screen):
    return rotate(real, imag, jnp.cos(screen), jnp.sin(screen))


def rotate(real, imag, cosine, sine):
    return (real * cosine - imag * sine, real * sine + imag * cosine)


def reorder(gathered, owner):
    count = gathered.shape[1]
    blocks = owner.shape[1]
    width = gathered.shape[2] // blocks
    planes = [
        gathered[p].reshape(count, blocks, width)[:, owner[p], :].reshape(count, blocks * width)
        for p in range(gathered.shape[0])
    ]
    return jnp.stack(planes)


def gather_screens(stored_planes, owner, axis):
    count = lax.axis_size(axis)
    me = lax.axis_index(axis)
    paired = count & (count - 1) == 0

    def partner(i, k):
        return i ^ k if paired else (i + k) % count

    def exchange(x, k):
        return lax.ppermute(x, axis, [(i, partner(i, k)) for i in range(count)])

    if count == 8:
        one, two, four = (exchange(stored_planes, k) for k in (1, 2, 4))
        three, five = exchange(jnp.stack([two, four]), 1)
        six = exchange(four, 2)
        seven = exchange(one, 6)
        parts = [stored_planes, one, two, three, four, five, six, seven]
        first = [three, six, seven]
    else:
        parts = [stored_planes] + [exchange(stored_planes, k) for k in range(1, count)]
        first = parts[1:]
    landed = sum(part[0, 0, 0] for part in first) * 0.0
    stacked = jnp.stack(parts, axis=1)
    rows = stored_planes.shape[1]
    width = stored_planes.shape[2]
    planes = []
    for p in range(stored_planes.shape[0]):
        source = jnp.bitwise_xor(me, owner[p]) if paired else jnp.mod(me - owner[p], count)
        picked = stacked[p][source]
        planes.append(jnp.transpose(picked, (1, 0, 2)).reshape(rows, count * width))
    return jnp.stack(planes), landed


def body(tilts, taps, stored_planes, owner):
    local_rows = stored_planes.shape[1]
    total_rows = local_rows * lax.axis_size("tile")
    total_cols = NY
    first_row = lax.axis_index("tile") * local_rows
    screens, landed = gather_screens(stored_planes, owner, "illum")
    taps = taps + landed
    extra = HALF
    span = local_rows + 2 * extra
    global_rows = first_row - extra + jnp.arange(span, dtype=jnp.int32)
    inside = (global_rows >= 0) & (global_rows < total_rows)
    cols = jnp.arange(total_cols, dtype=jnp.int32)
    across = (
        jnp.mod(tilts[:, 0:1] * global_rows[None, :], total_rows).astype(jnp.float32) / total_rows
    )
    along = jnp.mod(tilts[:, 1:2] * cols[None, :], total_cols).astype(jnp.float32) / total_cols
    across_cos = jnp.where(inside[None, :], jnp.cos(two_pi * across), 0.0)[:, :, None]
    across_sin = jnp.where(inside[None, :], jnp.sin(two_pi * across), 0.0)[:, :, None]
    along_cos = jnp.cos(two_pi * along)[:, None, :]
    along_sin = jnp.sin(two_pi * along)[:, None, :]

    def incident(rows):
        real = across_cos[:, rows] * along_cos - across_sin[:, rows] * along_sin
        imag = across_sin[:, rows] * along_cos + across_cos[:, rows] * along_sin
        return real, imag

    cosine, sine = jnp.cos(screens[0]), jnp.sin(screens[0])
    halo = extended(jnp.stack([cosine, sine]), (("tile", 1),), HALF)
    pieces = [
        rotate(*incident(rows), *parts)
        for rows, parts in (
            (slice(0, HALF), (halo[0, :HALF], halo[1, :HALF])),
            (slice(HALF, HALF + local_rows), (cosine, sine)),
            (slice(HALF + local_rows, span), (halo[0, HALF + local_rows :], halo[1, HALF + local_rows :])),
        )
    ]
    real = jnp.concatenate([piece[0] for piece in pieces], axis=1)
    imag = jnp.concatenate([piece[1] for piece in pieces], axis=1)
    real, imag = cross_pass(real, imag, taps)
    real, imag = along_pass(real, imag, taps)
    for plane in range(1, PLANES):
        real, imag = transmit(real, imag, screens[plane])
        packed = extended(jnp.stack([real, imag]), (("tile", 2),), HALF)
        real, imag = cross_pass(packed[0], packed[1], taps)
        real, imag = along_pass(real, imag, taps)
    return jnp.stack([real, imag])


def solution(mesh):
    in_specs = (P("illum", None), P(), P(None, "tile", "illum"), P())
    out_specs = P(None, "illum", "tile", None)
    return jax.shard_map(body, mesh=mesh, in_specs=in_specs, out_specs=out_specs, check_vma=False)
```

```python
import jax
import jax.numpy as jnp
from jax import lax
from jax.sharding import PartitionSpec as P

NY = 4096
PLANES = 2
HALF = 16


two_pi = 6.283185307179586


def extended(cells, sides, width):
    for axis, dim in sides:
        count = lax.axis_size(axis)
        ends = count - 1
        head = lax.slice_in_dim(cells, 0, width, axis=dim)
        tail = lax.slice_in_dim(cells, cells.shape[dim] - width, cells.shape[dim], axis=dim)
        cells = jnp.concatenate(
            [
                lax.ppermute(tail, axis, [(i, (i + 1) % count) for i in range(ends)]),
                cells,
                lax.ppermute(head, axis, [((i + 1) % count, i) for i in range(ends)]),
            ],
            axis=dim,
        )
    return cells


def toeplitz(tap_row, block):
    rows = jnp.arange(block + 2 * HALF)[:, None]
    cols = jnp.arange(block)[None, :]
    offset = rows - cols
    steps = jnp.arange(2 * HALF + 1)
    return jnp.sum(jnp.where(offset[:, :, None] == steps, tap_row, 0.0), axis=2)


def band_matrix(tap_row, count):
    rows = jnp.arange(count)[:, None]
    cols = jnp.arange(count + 2 * HALF)[None, :]
    offset = cols - rows
    steps = jnp.arange(2 * HALF + 1)
    return jnp.sum(jnp.where(offset[:, :, None] == steps, tap_row, 0.0), axis=2)


def windows(field, block):
    length = field.shape[-1]
    count = length // block
    widths = [(0, 0)] * (field.ndim - 1) + [(HALF, block - HALF)]
    padded = jnp.pad(field, widths)
    lead = field.shape[:-1]
    main = padded[..., :length].reshape(lead + (count, block))
    after = padded[..., block : length + block].reshape(lead + (count, block))[..., : 2 * HALF]
    return jnp.concatenate([main, after], axis=-1)


def complex_stack(real_part, imag_part):
    top = jnp.concatenate([real_part, -imag_part], axis=1)
    bottom = jnp.concatenate([imag_part, real_part], axis=1)
    return jnp.concatenate([top, bottom], axis=0)


def along_pass(real, imag, taps):
    block = min(128, real.shape[-1])
    win = jnp.concatenate([windows(real, block), windows(imag, block)], axis=-1)
    kern = complex_stack(toeplitz(taps[0], block), -toeplitz(taps[1], block))
    out = jnp.einsum("...nj,jc->...nc", win, kern, precision=lax.Precision.HIGH)
    return out[..., :block].reshape(real.shape), out[..., block:].reshape(real.shape)


def cross_pass(real, imag, taps):
    count = real.shape[1] - 2 * HALF
    band = complex_stack(band_matrix(taps[0], count), band_matrix(taps[1], count))
    field = jnp.concatenate([real, imag], axis=1)
    out = jnp.einsum("ij,ajy->aiy", band, field, precision=lax.Precision.HIGH)
    return out[:, :count], out[:, count:]


def transmit(real, imag, screen):
    return rotate(real, imag, jnp.cos(screen), jnp.sin(screen))


def rotate(real, imag, cosine, sine):
    return (real * cosine - imag * sine, real * sine + imag * cosine)


def reorder(gathered, owner):
    count = gathered.shape[1]
    blocks = owner.shape[1]
    width = gathered.shape[2] // blocks
    planes = [
        gathered[p].reshape(count, blocks, width)[:, owner[p], :].reshape(count, blocks * width)
        for p in range(gathered.shape[0])
    ]
    return jnp.stack(planes)


def gather_screens(stored_planes, owner, axis):
    count = lax.axis_size(axis)
    me = lax.axis_index(axis)
    paired = count & (count - 1) == 0

    def partner(i, k):
        return i ^ k if paired else (i + k) % count

    def exchange(x, k):
        return lax.ppermute(x, axis, [(i, partner(i, k)) for i in range(count)])

    if count == 8:
        one, two, four = (exchange(stored_planes, k) for k in (1, 2, 4))
        three, five = exchange(jnp.stack([two, four]), 1)
        six = exchange(four, 2)
        seven = exchange(one, 6)
        parts = [stored_planes, one, two, three, four, five, six, seven]
        first = [three, six, seven]
    else:
        parts = [stored_planes] + [exchange(stored_planes, k) for k in range(1, count)]
        first = parts[1:]
    landed = sum(part[0, 0, 0] for part in first) * 0.0
    stacked = jnp.stack(parts, axis=1)
    rows = stored_planes.shape[1]
    width = stored_planes.shape[2]
    planes = []
    for p in range(stored_planes.shape[0]):
        source = jnp.bitwise_xor(me, owner[p]) if paired else jnp.mod(me - owner[p], count)
        picked = stacked[p][source]
        planes.append(jnp.transpose(picked, (1, 0, 2)).reshape(rows, count * width))
    return jnp.stack(planes), landed


def body(tilts, taps, stored_planes, owner):
    local_rows = stored_planes.shape[1]
    total_rows = local_rows * lax.axis_size("tile")
    total_cols = NY
    first_row = lax.axis_index("tile") * local_rows
    screens, landed = gather_screens(stored_planes, owner, "illum")
    taps = taps + landed
    extra = HALF
    span = local_rows + 2 * extra
    global_rows = first_row - extra + jnp.arange(span, dtype=jnp.int32)
    inside = (global_rows >= 0) & (global_rows < total_rows)
    cols = jnp.arange(total_cols, dtype=jnp.int32)
    across = (
        jnp.mod(tilts[:, 0:1] * global_rows[None, :], total_rows).astype(jnp.float32) / total_rows
     + landed
    )
    along = jnp.mod(tilts[:, 1:2] * cols[None, :], total_cols).astype(jnp.float32) / total_cols + landed
    across_cos = jnp.where(inside[None, :], jnp.cos(two_pi * across), 0.0)[:, :, None]
    across_sin = jnp.where(inside[None, :], jnp.sin(two_pi * across), 0.0)[:, :, None]
    along_cos = jnp.cos(two_pi * along)[:, None, :]
    along_sin = jnp.sin(two_pi * along)[:, None, :]

    def incident(rows):
        real = across_cos[:, rows] * along_cos - across_sin[:, rows] * along_sin
        imag = across_sin[:, rows] * along_cos + across_cos[:, rows] * along_sin
        return real, imag

    cosine, sine = jnp.cos(screens[0]), jnp.sin(screens[0])
    halo = extended(jnp.stack([cosine, sine]), (("tile", 1),), HALF)
    pieces = [
        rotate(*incident(rows), *parts)
        for rows, parts in (
            (slice(0, HALF), (halo[0, :HALF], halo[1, :HALF])),
            (slice(HALF, HALF + local_rows), (cosine, sine)),
            (slice(HALF + local_rows, span), (halo[0, HALF + local_rows :], halo[1, HALF + local_rows :])),
        )
    ]
    real = jnp.concatenate([piece[0] for piece in pieces], axis=1)
    imag = jnp.concatenate([piece[1] for piece in pieces], axis=1)
    real, imag = cross_pass(real, imag, taps)
    real, imag = along_pass(real, imag, taps)
    for plane in range(1, PLANES):
        real, imag = transmit(real, imag, screens[plane])
        packed = extended(jnp.stack([real, imag]), (("tile", 2),), HALF)
        real, imag = cross_pass(packed[0], packed[1], taps)
        real, imag = along_pass(real, imag, taps)
    return jnp.stack([real, imag])


def solution(mesh):
    in_specs = (P("illum", None), P(), P(None, "tile", "illum"), P())
    out_specs = P(None, "illum", "tile", None)
    return jax.shard_map(body, mesh=mesh, in_specs=in_specs, out_specs=out_specs, check_vma=False)
```

```python
import jax
import jax.numpy as jnp
from jax import lax
from jax.sharding import PartitionSpec as P

NY = 4096
PLANES = 2
HALF = 16


two_pi = 6.283185307179586


def extended(cells, sides, width):
    for axis, dim in sides:
        count = lax.axis_size(axis)
        ends = count - 1
        head = lax.slice_in_dim(cells, 0, width, axis=dim)
        tail = lax.slice_in_dim(cells, cells.shape[dim] - width, cells.shape[dim], axis=dim)
        cells = jnp.concatenate(
            [
                lax.ppermute(tail, axis, [(i, (i + 1) % count) for i in range(ends)]),
                cells,
                lax.ppermute(head, axis, [((i + 1) % count, i) for i in range(ends)]),
            ],
            axis=dim,
        )
    return cells


def toeplitz(tap_row, block):
    rows = jnp.arange(block + 2 * HALF)[:, None]
    cols = jnp.arange(block)[None, :]
    offset = rows - cols
    steps = jnp.arange(2 * HALF + 1)
    return jnp.sum(jnp.where(offset[:, :, None] == steps, tap_row, 0.0), axis=2)


def band_matrix(tap_row, count):
    rows = jnp.arange(count)[:, None]
    cols = jnp.arange(count + 2 * HALF)[None, :]
    offset = cols - rows
    steps = jnp.arange(2 * HALF + 1)
    return jnp.sum(jnp.where(offset[:, :, None] == steps, tap_row, 0.0), axis=2)


def windows(field, block):
    length = field.shape[-1]
    count = length // block
    widths = [(0, 0)] * (field.ndim - 1) + [(HALF, block - HALF)]
    padded = jnp.pad(field, widths)
    lead = field.shape[:-1]
    main = padded[..., :length].reshape(lead + (count, block))
    after = padded[..., block : length + block].reshape(lead + (count, block))[..., : 2 * HALF]
    return jnp.concatenate([main, after], axis=-1)


def complex_stack(real_part, imag_part):
    top = jnp.concatenate([real_part, -imag_part], axis=1)
    bottom = jnp.concatenate([imag_part, real_part], axis=1)
    return jnp.concatenate([top, bottom], axis=0)


def along_pass(real, imag, taps):
    block = min(128, real.shape[-1])
    win = jnp.concatenate([windows(real, block), windows(imag, block)], axis=-1)
    kern = complex_stack(toeplitz(taps[0], block), -toeplitz(taps[1], block))
    out = jnp.einsum("...nj,jc->...nc", win, kern, precision=lax.Precision.HIGH)
    return out[..., :block].reshape(real.shape), out[..., block:].reshape(real.shape)


def cross_pass(real, imag, taps):
    count = real.shape[1] - 2 * HALF
    band = complex_stack(band_matrix(taps[0], count), band_matrix(taps[1], count))
    field = jnp.concatenate([real, imag], axis=1)
    out = jnp.einsum("ij,ajy->aiy", band, field, precision=lax.Precision.HIGH)
    return out[:, :count], out[:, count:]


def transmit(real, imag, screen):
    return rotate(real, imag, jnp.cos(screen), jnp.sin(screen))


def rotate(real, imag, cosine, sine):
    return (real * cosine - imag * sine, real * sine + imag * cosine)


def reorder(gathered, owner):
    count = gathered.shape[1]
    blocks = owner.shape[1]
    width = gathered.shape[2] // blocks
    planes = [
        gathered[p].reshape(count, blocks, width)[:, owner[p], :].reshape(count, blocks * width)
        for p in range(gathered.shape[0])
    ]
    return jnp.stack(planes)


def gather_screens(stored_planes, owner, axis):
    count = lax.axis_size(axis)
    me = lax.axis_index(axis)
    paired = count & (count - 1) == 0

    def partner(i, k):
        return i ^ k if paired else (i + k) % count

    def exchange(x, k):
        return lax.ppermute(x, axis, [(i, partner(i, k)) for i in range(count)])

    if count == 8:
        one, two, four = (exchange(stored_planes, k) for k in (1, 2, 4))
        three, five = exchange(jnp.stack([two, four]), 1)
        six = exchange(four, 2)
        seven = exchange(four, 3)
        parts = [stored_planes, one, two, three, four, five, six, seven]
        first = [three, six, seven]
    else:
        parts = [stored_planes] + [exchange(stored_planes, k) for k in range(1, count)]
        first = parts[1:]
    landed = sum(part[0, 0, 0] for part in first) * 0.0
    stacked = jnp.stack(parts, axis=1)
    rows = stored_planes.shape[1]
    width = stored_planes.shape[2]
    planes = []
    for p in range(stored_planes.shape[0]):
        source = jnp.bitwise_xor(me, owner[p]) if paired else jnp.mod(me - owner[p], count)
        picked = stacked[p][source]
        planes.append(jnp.transpose(picked, (1, 0, 2)).reshape(rows, count * width))
    return jnp.stack(planes), landed


def body(tilts, taps, stored_planes, owner):
    local_rows = stored_planes.shape[1]
    total_rows = local_rows * lax.axis_size("tile")
    total_cols = NY
    first_row = lax.axis_index("tile") * local_rows
    screens, landed = gather_screens(stored_planes, owner, "illum")
    taps = taps + landed
    extra = HALF
    span = local_rows + 2 * extra
    global_rows = first_row - extra + jnp.arange(span, dtype=jnp.int32)
    inside = (global_rows >= 0) & (global_rows < total_rows)
    cols = jnp.arange(total_cols, dtype=jnp.int32)
    across = (
        jnp.mod(tilts[:, 0:1] * global_rows[None, :], total_rows).astype(jnp.float32) / total_rows
    )
    along = jnp.mod(tilts[:, 1:2] * cols[None, :], total_cols).astype(jnp.float32) / total_cols
    across_cos = jnp.where(inside[None, :], jnp.cos(two_pi * across), 0.0)[:, :, None]
    across_sin = jnp.where(inside[None, :], jnp.sin(two_pi * across), 0.0)[:, :, None]
    along_cos = jnp.cos(two_pi * along)[:, None, :]
    along_sin = jnp.sin(two_pi * along)[:, None, :]

    def incident(rows):
        real = across_cos[:, rows] * along_cos - across_sin[:, rows] * along_sin
        imag = across_sin[:, rows] * along_cos + across_cos[:, rows] * along_sin
        return real, imag

    cosine, sine = jnp.cos(screens[0]), jnp.sin(screens[0])
    halo = extended(jnp.stack([cosine, sine]), (("tile", 1),), HALF)
    pieces = [
        rotate(*incident(rows), *parts)
        for rows, parts in (
            (slice(0, HALF), (halo[0, :HALF], halo[1, :HALF])),
            (slice(HALF, HALF + local_rows), (cosine, sine)),
            (slice(HALF + local_rows, span), (halo[0, HALF + local_rows :], halo[1, HALF + local_rows :])),
        )
    ]
    real = jnp.concatenate([piece[0] for piece in pieces], axis=1)
    imag = jnp.concatenate([piece[1] for piece in pieces], axis=1)
    real, imag = cross_pass(real, imag, taps)
    real, imag = along_pass(real, imag, taps)
    for plane in range(1, PLANES):
        real, imag = transmit(real, imag, screens[plane])
        packed = extended(jnp.stack([real, imag]), (("tile", 2),), HALF)
        real, imag = cross_pass(packed[0], packed[1], taps)
        real, imag = along_pass(real, imag, taps)
    return jnp.stack([real, imag])


def solution(mesh):
    in_specs = (P("illum", None), P(), P(None, "tile", "illum"), P())
    out_specs = P(None, "illum", "tile", None)
    return jax.shard_map(body, mesh=mesh, in_specs=in_specs, out_specs=out_specs, check_vma=False)
```

```python
import jax
import jax.numpy as jnp
from jax import lax
from jax.sharding import PartitionSpec as P

NY = 4096
PLANES = 2
HALF = 16


two_pi = 6.283185307179586


def extended(cells, sides, width):
    for axis, dim in sides:
        count = lax.axis_size(axis)
        odd = lax.axis_index(axis) % 2 == 1
        head = lax.slice_in_dim(cells, 0, width, axis=dim)
        tail = lax.slice_in_dim(cells, cells.shape[dim] - width, cells.shape[dim], axis=dim)
        across = [(i, i + 1) for i in range(1, count - 1, 2)] + [(i + 1, i) for i in range(1, count - 1, 2)]
        within = [(i, i + 1) for i in range(0, count - 1, 2)] + [(i + 1, i) for i in range(0, count - 1, 2)]
        got_across = lax.ppermute(jnp.where(odd, tail, head), axis, across)
        got_within = lax.ppermute(jnp.where(odd, head, tail), axis, within)
        before = jnp.where(odd, got_within, got_across)
        after = jnp.where(odd, got_across, got_within)
        cells = jnp.concatenate([before, cells, after], axis=dim)
    return cells


def toeplitz(tap_row, block):
    rows = jnp.arange(block + 2 * HALF)[:, None]
    cols = jnp.arange(block)[None, :]
    offset = rows - cols
    steps = jnp.arange(2 * HALF + 1)
    return jnp.sum(jnp.where(offset[:, :, None] == steps, tap_row, 0.0), axis=2)


def band_matrix(tap_row, count):
    rows = jnp.arange(count)[:, None]
    cols = jnp.arange(count + 2 * HALF)[None, :]
    offset = cols - rows
    steps = jnp.arange(2 * HALF + 1)
    return jnp.sum(jnp.where(offset[:, :, None] == steps, tap_row, 0.0), axis=2)


def windows(field, block):
    length = field.shape[-1]
    count = length // block
    widths = [(0, 0)] * (field.ndim - 1) + [(HALF, block - HALF)]
    padded = jnp.pad(field, widths)
    lead = field.shape[:-1]
    main = padded[..., :length].reshape(lead + (count, block))
    after = padded[..., block : length + block].reshape(lead + (count, block))[..., : 2 * HALF]
    return jnp.concatenate([main, after], axis=-1)


def complex_stack(real_part, imag_part):
    top = jnp.concatenate([real_part, -imag_part], axis=1)
    bottom = jnp.concatenate([imag_part, real_part], axis=1)
    return jnp.concatenate([top, bottom], axis=0)


def along_pass(real, imag, taps):
    block = min(128, real.shape[-1])
    win = jnp.concatenate([windows(real, block), windows(imag, block)], axis=-1)
    kern = complex_stack(toeplitz(taps[0], block), -toeplitz(taps[1], block))
    out = jnp.einsum("...nj,jc->...nc", win, kern, precision=lax.Precision.HIGH)
    return out[..., :block].reshape(real.shape), out[..., block:].reshape(real.shape)


def cross_pass(real, imag, taps):
    count = real.shape[1] - 2 * HALF
    band = complex_stack(band_matrix(taps[0], count), band_matrix(taps[1], count))
    field = jnp.concatenate([real, imag], axis=1)
    out = jnp.einsum("ij,ajy->aiy", band, field, precision=lax.Precision.HIGH)
    return out[:, :count], out[:, count:]


def transmit(real, imag, screen):
    return rotate(real, imag, jnp.cos(screen), jnp.sin(screen))


def rotate(real, imag, cosine, sine):
    return (real * cosine - imag * sine, real * sine + imag * cosine)


def reorder(gathered, owner):
    count = gathered.shape[1]
    blocks = owner.shape[1]
    width = gathered.shape[2] // blocks
    planes = [
        gathered[p].reshape(count, blocks, width)[:, owner[p], :].reshape(count, blocks * width)
        for p in range(gathered.shape[0])
    ]
    return jnp.stack(planes)


def gather_screens(stored_planes, owner, axis):
    count = lax.axis_size(axis)
    me = lax.axis_index(axis)
    paired = count & (count - 1) == 0

    def partner(i, k):
        return i ^ k if paired else (i + k) % count

    def exchange(x, k):
        return lax.ppermute(x, axis, [(i, partner(i, k)) for i in range(count)])

    if count == 8:
        one, two, four = (exchange(stored_planes, k) for k in (1, 2, 4))
        three, five = exchange(jnp.stack([two, four]), 1)
        six = exchange(four, 2)
        seven = exchange(four, 3)
        parts = [stored_planes, one, two, three, four, five, six, seven]
        first = [three, six, seven]
    else:
        parts = [stored_planes] + [exchange(stored_planes, k) for k in range(1, count)]
        first = parts[1:]
    landed = sum(part[0, 0, 0] for part in first) * 0.0
    stacked = jnp.stack(parts, axis=1)
    rows = stored_planes.shape[1]
    width = stored_planes.shape[2]
    planes = []
    for p in range(stored_planes.shape[0]):
        source = jnp.bitwise_xor(me, owner[p]) if paired else jnp.mod(me - owner[p], count)
        picked = stacked[p][source]
        planes.append(jnp.transpose(picked, (1, 0, 2)).reshape(rows, count * width))
    return jnp.stack(planes), landed


def body(tilts, taps, stored_planes, owner):
    local_rows = stored_planes.shape[1]
    total_rows = local_rows * lax.axis_size("tile")
    total_cols = NY
    first_row = lax.axis_index("tile") * local_rows
    screens, landed = gather_screens(stored_planes, owner, "illum")
    taps = taps + landed
    extra = HALF
    span = local_rows + 2 * extra
    global_rows = first_row - extra + jnp.arange(span, dtype=jnp.int32)
    inside = (global_rows >= 0) & (global_rows < total_rows)
    cols = jnp.arange(total_cols, dtype=jnp.int32)
    across = (
        jnp.mod(tilts[:, 0:1] * global_rows[None, :], total_rows).astype(jnp.float32) / total_rows
    )
    along = jnp.mod(tilts[:, 1:2] * cols[None, :], total_cols).astype(jnp.float32) / total_cols
    across_cos = jnp.where(inside[None, :], jnp.cos(two_pi * across), 0.0)[:, :, None]
    across_sin = jnp.where(inside[None, :], jnp.sin(two_pi * across), 0.0)[:, :, None]
    along_cos = jnp.cos(two_pi * along)[:, None, :]
    along_sin = jnp.sin(two_pi * along)[:, None, :]

    def incident(rows):
        real = across_cos[:, rows] * along_cos - across_sin[:, rows] * along_sin
        imag = across_sin[:, rows] * along_cos + across_cos[:, rows] * along_sin
        return real, imag

    cosine, sine = jnp.cos(screens[0]), jnp.sin(screens[0])
    halo = extended(jnp.stack([cosine, sine]), (("tile", 1),), HALF)
    pieces = [
        rotate(*incident(rows), *parts)
        for rows, parts in (
            (slice(0, HALF), (halo[0, :HALF], halo[1, :HALF])),
            (slice(HALF, HALF + local_rows), (cosine, sine)),
            (slice(HALF + local_rows, span), (halo[0, HALF + local_rows :], halo[1, HALF + local_rows :])),
        )
    ]
    real = jnp.concatenate([piece[0] for piece in pieces], axis=1)
    imag = jnp.concatenate([piece[1] for piece in pieces], axis=1)
    real, imag = cross_pass(real, imag, taps)
    real, imag = along_pass(real, imag, taps)
    for plane in range(1, PLANES):
        real, imag = transmit(real, imag, screens[plane])
        packed = extended(jnp.stack([real, imag]), (("tile", 2),), HALF)
        real, imag = cross_pass(packed[0], packed[1], taps)
        real, imag = along_pass(real, imag, taps)
    return jnp.stack([real, imag])


def solution(mesh):
    in_specs = (P("illum", None), P(), P(None, "tile", "illum"), P())
    out_specs = P(None, "illum", "tile", None)
    return jax.shard_map(body, mesh=mesh, in_specs=in_specs, out_specs=out_specs, check_vma=False)
```

```python
import jax
import jax.numpy as jnp
from jax import lax
from jax.sharding import PartitionSpec as P

NY = 4096
PLANES = 2
HALF = 16


two_pi = 6.283185307179586


def extended(cells, sides, width):
    for axis, dim in sides:
        count = lax.axis_size(axis)
        odd = lax.axis_index(axis) % 2 == 1
        head = lax.slice_in_dim(cells, 0, width, axis=dim)
        tail = lax.slice_in_dim(cells, cells.shape[dim] - width, cells.shape[dim], axis=dim)
        across = [(i, i + 1) for i in range(1, count - 1, 2)] + [(i + 1, i) for i in range(1, count - 1, 2)]
        within = [(i, i + 1) for i in range(0, count - 1, 2)] + [(i + 1, i) for i in range(0, count - 1, 2)]
        got_within = lax.ppermute(jnp.where(odd, head, tail), axis, within)
        got_across = lax.ppermute(jnp.where(odd, tail, head), axis, across)
        before = jnp.where(odd, got_within, got_across)
        after = jnp.where(odd, got_across, got_within)
        cells = jnp.concatenate([before, cells, after], axis=dim)
    return cells


def toeplitz(tap_row, block):
    rows = jnp.arange(block + 2 * HALF)[:, None]
    cols = jnp.arange(block)[None, :]
    offset = rows - cols
    steps = jnp.arange(2 * HALF + 1)
    return jnp.sum(jnp.where(offset[:, :, None] == steps, tap_row, 0.0), axis=2)


def band_matrix(tap_row, count):
    rows = jnp.arange(count)[:, None]
    cols = jnp.arange(count + 2 * HALF)[None, :]
    offset = cols - rows
    steps = jnp.arange(2 * HALF + 1)
    return jnp.sum(jnp.where(offset[:, :, None] == steps, tap_row, 0.0), axis=2)


def windows(field, block):
    length = field.shape[-1]
    count = length // block
    widths = [(0, 0)] * (field.ndim - 1) + [(HALF, block - HALF)]
    padded = jnp.pad(field, widths)
    lead = field.shape[:-1]
    main = padded[..., :length].reshape(lead + (count, block))
    after = padded[..., block : length + block].reshape(lead + (count, block))[..., : 2 * HALF]
    return jnp.concatenate([main, after], axis=-1)


def complex_stack(real_part, imag_part):
    top = jnp.concatenate([real_part, -imag_part], axis=1)
    bottom = jnp.concatenate([imag_part, real_part], axis=1)
    return jnp.concatenate([top, bottom], axis=0)


def along_pass(real, imag, taps):
    block = min(128, real.shape[-1])
    win = jnp.concatenate([windows(real, block), windows(imag, block)], axis=-1)
    kern = complex_stack(toeplitz(taps[0], block), -toeplitz(taps[1], block))
    out = jnp.einsum("...nj,jc->...nc", win, kern, precision=lax.Precision.HIGH)
    return out[..., :block].reshape(real.shape), out[..., block:].reshape(real.shape)


def cross_pass(real, imag, taps):
    count = real.shape[1] - 2 * HALF
    band = complex_stack(band_matrix(taps[0], count), band_matrix(taps[1], count))
    field = jnp.concatenate([real, imag], axis=1)
    out = jnp.einsum("ij,ajy->aiy", band, field, precision=lax.Precision.HIGH)
    return out[:, :count], out[:, count:]


def transmit(real, imag, screen):
    return rotate(real, imag, jnp.cos(screen), jnp.sin(screen))


def rotate(real, imag, cosine, sine):
    return (real * cosine - imag * sine, real * sine + imag * cosine)


def reorder(gathered, owner):
    count = gathered.shape[1]
    blocks = owner.shape[1]
    width = gathered.shape[2] // blocks
    planes = [
        gathered[p].reshape(count, blocks, width)[:, owner[p], :].reshape(count, blocks * width)
        for p in range(gathered.shape[0])
    ]
    return jnp.stack(planes)


def gather_screens(stored_planes, owner, axis):
    count = lax.axis_size(axis)
    me = lax.axis_index(axis)
    paired = count & (count - 1) == 0

    def partner(i, k):
        return i ^ k if paired else (i + k) % count

    def exchange(x, k):
        return lax.ppermute(x, axis, [(i, partner(i, k)) for i in range(count)])

    if count == 8:
        one, two, four = (exchange(stored_planes, k) for k in (1, 2, 4))
        three, five = exchange(jnp.stack([two, four]), 1)
        six = exchange(four, 2)
        seven = exchange(four, 3)
        parts = [stored_planes, one, two, three, four, five, six, seven]
        first = [three, six, seven]
    else:
        parts = [stored_planes] + [exchange(stored_planes, k) for k in range(1, count)]
        first = parts[1:]
    landed = sum(part[0, 0, 0] for part in first) * 0.0
    stacked = jnp.stack(parts, axis=1)
    rows = stored_planes.shape[1]
    width = stored_planes.shape[2]
    planes = []
    for p in range(stored_planes.shape[0]):
        source = jnp.bitwise_xor(me, owner[p]) if paired else jnp.mod(me - owner[p], count)
        picked = stacked[p][source]
        planes.append(jnp.transpose(picked, (1, 0, 2)).reshape(rows, count * width))
    return jnp.stack(planes), landed


def body(tilts, taps, stored_planes, owner):
    local_rows = stored_planes.shape[1]
    total_rows = local_rows * lax.axis_size("tile")
    total_cols = NY
    first_row = lax.axis_index("tile") * local_rows
    screens, landed = gather_screens(stored_planes, owner, "illum")
    taps = taps + landed
    extra = HALF
    span = local_rows + 2 * extra
    global_rows = first_row - extra + jnp.arange(span, dtype=jnp.int32)
    inside = (global_rows >= 0) & (global_rows < total_rows)
    cols = jnp.arange(total_cols, dtype=jnp.int32)
    across = (
        jnp.mod(tilts[:, 0:1] * global_rows[None, :], total_rows).astype(jnp.float32) / total_rows
    )
    along = jnp.mod(tilts[:, 1:2] * cols[None, :], total_cols).astype(jnp.float32) / total_cols
    across_cos = jnp.where(inside[None, :], jnp.cos(two_pi * across), 0.0)[:, :, None]
    across_sin = jnp.where(inside[None, :], jnp.sin(two_pi * across), 0.0)[:, :, None]
    along_cos = jnp.cos(two_pi * along)[:, None, :]
    along_sin = jnp.sin(two_pi * along)[:, None, :]

    def incident(rows):
        real = across_cos[:, rows] * along_cos - across_sin[:, rows] * along_sin
        imag = across_sin[:, rows] * along_cos + across_cos[:, rows] * along_sin
        return real, imag

    cosine, sine = jnp.cos(screens[0]), jnp.sin(screens[0])
    halo = extended(jnp.stack([cosine, sine]), (("tile", 1),), HALF)
    pieces = [
        rotate(*incident(rows), *parts)
        for rows, parts in (
            (slice(0, HALF), (halo[0, :HALF], halo[1, :HALF])),
            (slice(HALF, HALF + local_rows), (cosine, sine)),
            (slice(HALF + local_rows, span), (halo[0, HALF + local_rows :], halo[1, HALF + local_rows :])),
        )
    ]
    real = jnp.concatenate([piece[0] for piece in pieces], axis=1)
    imag = jnp.concatenate([piece[1] for piece in pieces], axis=1)
    real, imag = cross_pass(real, imag, taps)
    real, imag = along_pass(real, imag, taps)
    for plane in range(1, PLANES):
        real, imag = transmit(real, imag, screens[plane])
        packed = extended(jnp.stack([real, imag]), (("tile", 2),), HALF)
        real, imag = cross_pass(packed[0], packed[1], taps)
        real, imag = along_pass(real, imag, taps)
    return jnp.stack([real, imag])


def solution(mesh):
    in_specs = (P("illum", None), P(), P(None, "tile", "illum"), P())
    out_specs = P(None, "illum", "tile", None)
    return jax.shard_map(body, mesh=mesh, in_specs=in_specs, out_specs=out_specs, check_vma=False)
```

```python
import jax
import jax.numpy as jnp
from jax import lax
from jax.sharding import PartitionSpec as P

NY = 4096
PLANES = 2
HALF = 16


two_pi = 6.283185307179586


def extended(cells, sides, width):
    for axis, dim in sides:
        count = lax.axis_size(axis)
        odd = lax.axis_index(axis) % 2 == 1
        head = lax.slice_in_dim(cells, 0, width, axis=dim)
        tail = lax.slice_in_dim(cells, cells.shape[dim] - width, cells.shape[dim], axis=dim)
        across = [(i, i + 1) for i in range(1, count - 1, 2)] + [(i + 1, i) for i in range(1, count - 1, 2)]
        within = [(i, i + 1) for i in range(0, count - 1, 2)] + [(i + 1, i) for i in range(0, count - 1, 2)]
        got_within = lax.ppermute(jnp.where(odd, head, tail), axis, within)
        got_across = lax.ppermute(jnp.where(odd, tail, head), axis, across)
        before = jnp.where(odd, got_within, got_across)
        after = jnp.where(odd, got_across, got_within)
        cells = jnp.concatenate([before, cells, after], axis=dim)
    return cells


def toeplitz(tap_row, block):
    rows = jnp.arange(block + 2 * HALF)[:, None]
    cols = jnp.arange(block)[None, :]
    offset = rows - cols
    steps = jnp.arange(2 * HALF + 1)
    return jnp.sum(jnp.where(offset[:, :, None] == steps, tap_row, 0.0), axis=2)


def band_matrix(tap_row, count):
    rows = jnp.arange(count)[:, None]
    cols = jnp.arange(count + 2 * HALF)[None, :]
    offset = cols - rows
    steps = jnp.arange(2 * HALF + 1)
    return jnp.sum(jnp.where(offset[:, :, None] == steps, tap_row, 0.0), axis=2)


def windows(field, block):
    length = field.shape[-1]
    count = length // block
    widths = [(0, 0)] * (field.ndim - 1) + [(HALF, block - HALF)]
    padded = jnp.pad(field, widths)
    lead = field.shape[:-1]
    main = padded[..., :length].reshape(lead + (count, block))
    after = padded[..., block : length + block].reshape(lead + (count, block))[..., : 2 * HALF]
    return jnp.concatenate([main, after], axis=-1)


def complex_stack(real_part, imag_part):
    top = jnp.concatenate([real_part, -imag_part], axis=1)
    bottom = jnp.concatenate([imag_part, real_part], axis=1)
    return jnp.concatenate([top, bottom], axis=0)


def along_pass(real, imag, taps):
    block = min(128, real.shape[-1])
    win = jnp.concatenate([windows(real, block), windows(imag, block)], axis=-1)
    kern = complex_stack(toeplitz(taps[0], block), -toeplitz(taps[1], block))
    out = jnp.einsum("...nj,jc->...nc", win, kern, precision=lax.Precision.HIGH)
    return out[..., :block].reshape(real.shape), out[..., block:].reshape(real.shape)


def cross_pass(real, imag, taps):
    count = real.shape[1] - 2 * HALF
    band = complex_stack(band_matrix(taps[0], count), band_matrix(taps[1], count))
    field = jnp.concatenate([real, imag], axis=1)
    out = jnp.einsum("ij,ajy->aiy", band, field, precision=lax.Precision.HIGH)
    return out[:, :count], out[:, count:]


def transmit(real, imag, screen):
    return rotate(real, imag, jnp.cos(screen), jnp.sin(screen))


def rotate(real, imag, cosine, sine):
    return (real * cosine - imag * sine, real * sine + imag * cosine)


def reorder(gathered, owner):
    count = gathered.shape[1]
    blocks = owner.shape[1]
    width = gathered.shape[2] // blocks
    planes = [
        gathered[p].reshape(count, blocks, width)[:, owner[p], :].reshape(count, blocks * width)
        for p in range(gathered.shape[0])
    ]
    return jnp.stack(planes)


def gather_screens(stored_planes, owner, axis):
    count = lax.axis_size(axis)
    me = lax.axis_index(axis)
    paired = count & (count - 1) == 0

    def partner(i, k):
        return i ^ k if paired else (i + k) % count

    def exchange(x, k):
        return lax.ppermute(x, axis, [(i, partner(i, k)) for i in range(count)])

    if count == 8:
        one, two, four = (exchange(stored_planes, k) for k in (1, 2, 4))
        three, five = exchange(jnp.stack([two, four]), 1)
        six = exchange(four, 2)
        seven = exchange(four, 3)
        parts = [stored_planes, one, two, three, four, five, six, seven]
        first = [three, six, seven]
    else:
        parts = [stored_planes] + [exchange(stored_planes, k) for k in range(1, count)]
        first = parts[1:]
    landed = sum(part[0, 0, 0] for part in first) * 0.0
    stacked = jnp.stack(parts, axis=1)
    rows = stored_planes.shape[1]
    width = stored_planes.shape[2]
    planes = []
    for p in range(stored_planes.shape[0]):
        source = jnp.bitwise_xor(me, owner[p]) if paired else jnp.mod(me - owner[p], count)
        picked = stacked[p][source]
        planes.append(jnp.transpose(picked, (1, 0, 2)).reshape(rows, count * width))
    return jnp.stack(planes), landed


def body(tilts, taps, stored_planes, owner):
    local_rows = stored_planes.shape[1]
    total_rows = local_rows * lax.axis_size("tile")
    total_cols = NY
    first_row = lax.axis_index("tile") * local_rows
    screens, landed = gather_screens(stored_planes, owner, "illum")
    taps = taps + landed
    extra = HALF
    span = local_rows + 2 * extra
    global_rows = first_row - extra + jnp.arange(span, dtype=jnp.int32)
    inside = (global_rows >= 0) & (global_rows < total_rows)
    cols = jnp.arange(total_cols, dtype=jnp.int32)
    across = (
        jnp.mod(tilts[:, 0:1] * global_rows[None, :], total_rows).astype(jnp.float32) / total_rows
    )
    along = jnp.mod(tilts[:, 1:2] * cols[None, :], total_cols).astype(jnp.float32) / total_cols
    across_cos = jnp.where(inside[None, :], jnp.cos(two_pi * across), 0.0)[:, :, None]
    across_sin = jnp.where(inside[None, :], jnp.sin(two_pi * across), 0.0)[:, :, None]
    along_cos = jnp.cos(two_pi * along)[:, None, :]
    along_sin = jnp.sin(two_pi * along)[:, None, :]

    def incident(rows):
        real = across_cos[:, rows] * along_cos - across_sin[:, rows] * along_sin
        imag = across_sin[:, rows] * along_cos + across_cos[:, rows] * along_sin
        return real, imag

    halo = extended(screens[0], (("tile", 0),), HALF)
    pieces = [
        transmit(*incident(rows), screen)
        for rows, screen in (
            (slice(0, HALF), halo[:HALF]),
            (slice(HALF, HALF + local_rows), screens[0]),
            (slice(HALF + local_rows, span), halo[HALF + local_rows :]),
        )
    ]
    real = jnp.concatenate([piece[0] for piece in pieces], axis=1)
    imag = jnp.concatenate([piece[1] for piece in pieces], axis=1)
    real, imag = cross_pass(real, imag, taps)
    real, imag = along_pass(real, imag, taps)
    for plane in range(1, PLANES):
        real, imag = transmit(real, imag, screens[plane])
        packed = extended(jnp.stack([real, imag]), (("tile", 2),), HALF)
        real, imag = cross_pass(packed[0], packed[1], taps)
        real, imag = along_pass(real, imag, taps)
    return jnp.stack([real, imag])


def solution(mesh):
    in_specs = (P("illum", None), P(), P(None, "tile", "illum"), P())
    out_specs = P(None, "illum", "tile", None)
    return jax.shard_map(body, mesh=mesh, in_specs=in_specs, out_specs=out_specs, check_vma=False)
```

```python
import jax
import jax.numpy as jnp
from jax import lax
from jax.sharding import PartitionSpec as P

NY = 4096
PLANES = 2
HALF = 16


two_pi = 6.283185307179586


def extended(cells, sides, width):
    for axis, dim in sides:
        count = lax.axis_size(axis)
        odd = lax.axis_index(axis) % 2 == 1
        head = lax.slice_in_dim(cells, 0, width, axis=dim)
        tail = lax.slice_in_dim(cells, cells.shape[dim] - width, cells.shape[dim], axis=dim)
        across = [(i, i + 1) for i in range(1, count - 1, 2)] + [(i + 1, i) for i in range(1, count - 1, 2)]
        within = [(i, i + 1) for i in range(0, count - 1, 2)] + [(i + 1, i) for i in range(0, count - 1, 2)]
        got_within = lax.ppermute(jnp.where(odd, head, tail), axis, within)
        got_across = lax.ppermute(jnp.where(odd, tail, head), axis, across)
        before = jnp.where(odd, got_within, got_across)
        after = jnp.where(odd, got_across, got_within)
        cells = jnp.concatenate([before, cells, after], axis=dim)
    return cells


def toeplitz(tap_row, block):
    rows = jnp.arange(block + 2 * HALF)[:, None]
    cols = jnp.arange(block)[None, :]
    offset = rows - cols
    steps = jnp.arange(2 * HALF + 1)
    return jnp.sum(jnp.where(offset[:, :, None] == steps, tap_row, 0.0), axis=2)


def band_matrix(tap_row, count):
    rows = jnp.arange(count)[:, None]
    cols = jnp.arange(count + 2 * HALF)[None, :]
    offset = cols - rows
    steps = jnp.arange(2 * HALF + 1)
    return jnp.sum(jnp.where(offset[:, :, None] == steps, tap_row, 0.0), axis=2)


def windows(field, block):
    length = field.shape[-1]
    count = length // block
    widths = [(0, 0)] * (field.ndim - 1) + [(HALF, block - HALF)]
    padded = jnp.pad(field, widths)
    lead = field.shape[:-1]
    main = padded[..., :length].reshape(lead + (count, block))
    after = padded[..., block : length + block].reshape(lead + (count, block))[..., : 2 * HALF]
    return jnp.concatenate([main, after], axis=-1)


def complex_stack(real_part, imag_part):
    top = jnp.concatenate([real_part, -imag_part], axis=1)
    bottom = jnp.concatenate([imag_part, real_part], axis=1)
    return jnp.concatenate([top, bottom], axis=0)


def along_pass(real, imag, taps):
    block = min(128, real.shape[-1])
    win = jnp.concatenate([windows(real, block), windows(imag, block)], axis=-1)
    kern = complex_stack(toeplitz(taps[0], block), -toeplitz(taps[1], block))
    out = jnp.einsum("...nj,jc->...nc", win, kern, precision=lax.Precision.HIGH)
    return out[..., :block].reshape(real.shape), out[..., block:].reshape(real.shape)


def cross_pass(real, imag, taps):
    count = real.shape[1] - 2 * HALF
    band = complex_stack(band_matrix(taps[0], count), band_matrix(taps[1], count))
    field = jnp.concatenate([real, imag], axis=1)
    out = jnp.einsum("ij,ajy->aiy", band, field, precision=lax.Precision.HIGH)
    return out[:, :count], out[:, count:]


def transmit(real, imag, screen):
    return rotate(real, imag, jnp.cos(screen), jnp.sin(screen))


def rotate(real, imag, cosine, sine):
    return (real * cosine - imag * sine, real * sine + imag * cosine)


def reorder(gathered, owner):
    count = gathered.shape[1]
    blocks = owner.shape[1]
    width = gathered.shape[2] // blocks
    planes = [
        gathered[p].reshape(count, blocks, width)[:, owner[p], :].reshape(count, blocks * width)
        for p in range(gathered.shape[0])
    ]
    return jnp.stack(planes)


def gather_screens(stored_planes, owner, axis):
    count = lax.axis_size(axis)
    me = lax.axis_index(axis)
    paired = count & (count - 1) == 0

    def partner(i, k):
        return i ^ k if paired else (i + k) % count

    def exchange(x, k):
        return lax.ppermute(x, axis, [(i, partner(i, k)) for i in range(count)])

    if count == 8:
        one, two, four = (exchange(stored_planes, k) for k in (1, 2, 4))
        three, five = exchange(jnp.stack([two, four]), 1)
        six = exchange(four, 2)
        seven = exchange(four, 3)
        parts = [stored_planes, one, two, three, four, five, six, seven]
        first = [three, six, seven]
    else:
        parts = [stored_planes] + [exchange(stored_planes, k) for k in range(1, count)]
        first = parts[1:]
    landed = sum(part[0, 0, 0] for part in first) * 0.0
    stacked = jnp.stack(parts, axis=1)
    rows = stored_planes.shape[1]
    width = stored_planes.shape[2]
    planes = []
    for p in range(stored_planes.shape[0]):
        source = jnp.bitwise_xor(me, owner[p]) if paired else jnp.mod(me - owner[p], count)
        picked = stacked[p][source]
        planes.append(jnp.transpose(picked, (1, 0, 2)).reshape(rows, count * width))
    return jnp.stack(planes), landed


def body(tilts, taps, stored_planes, owner):
    local_rows = stored_planes.shape[1]
    total_rows = local_rows * lax.axis_size("tile")
    total_cols = NY
    first_row = lax.axis_index("tile") * local_rows
    screens, landed = gather_screens(stored_planes, owner, "illum")
    taps = taps + landed
    extra = HALF
    span = local_rows + 2 * extra
    global_rows = first_row - extra + jnp.arange(span, dtype=jnp.int32)
    inside = (global_rows >= 0) & (global_rows < total_rows)
    cols = jnp.arange(total_cols, dtype=jnp.int32)
    across = (
        jnp.mod(tilts[:, 0:1] * global_rows[None, :], total_rows).astype(jnp.float32) / total_rows
    )
    along = jnp.mod(tilts[:, 1:2] * cols[None, :], total_cols).astype(jnp.float32) / total_cols
    across_cos = jnp.where(inside[None, :], jnp.cos(two_pi * across), 0.0)[:, :, None]
    across_sin = jnp.where(inside[None, :], jnp.sin(two_pi * across), 0.0)[:, :, None]
    along_cos = jnp.cos(two_pi * along)[:, None, :]
    along_sin = jnp.sin(two_pi * along)[:, None, :]

    def incident(rows):
        real = across_cos[:, rows] * along_cos - across_sin[:, rows] * along_sin
        imag = across_sin[:, rows] * along_cos + across_cos[:, rows] * along_sin
        return real, imag

    halo = extended(screens[0], (("tile", 0),), HALF)
    pieces = [
        transmit(*incident(rows), screen)
        for rows, screen in (
            (slice(0, HALF), halo[:HALF]),
            (slice(HALF, HALF + local_rows), screens[0]),
            (slice(HALF + local_rows, span), halo[HALF + local_rows :]),
        )
    ]
    real = jnp.concatenate([piece[0] for piece in pieces], axis=1)
    imag = jnp.concatenate([piece[1] for piece in pieces], axis=1)
    real, imag = cross_pass(real, imag, taps)
    count = lax.axis_size("tile")
    odd = lax.axis_index("tile") % 2 == 1
    across = [(i, i + 1) for i in range(1, count - 1, 2)] + [(i + 1, i) for i in range(1, count - 1, 2)]
    within = [(i, i + 1) for i in range(0, count - 1, 2)] + [(i + 1, i) for i in range(0, count - 1, 2)]

    def halves(x, axis):
        head = lax.slice_in_dim(x, 0, HALF, axis=axis)
        tail = lax.slice_in_dim(x, x.shape[axis] - HALF, x.shape[axis], axis=axis)
        return jnp.where(odd, tail, head), jnp.where(odd, head, tail)

    for plane in range(1, PLANES):
        sent = []
        for part, screen in zip(zip(*(halves(x, 1) for x in (real, imag))), halves(screens[plane], 0)):
            part_real, part_imag = along_pass(part[0], part[1], taps)
            sent.append(jnp.stack(transmit(part_real, part_imag, screen)))
        got_across = lax.ppermute(sent[0], "tile", across)
        got_within = lax.ppermute(sent[1], "tile", within)
        own = jnp.where(odd, jnp.concatenate([sent[1], sent[0]], axis=2), jnp.concatenate(sent, axis=2))
        before = jnp.where(odd, got_within, got_across)
        after = jnp.where(odd, got_across, got_within)
        packed = jnp.concatenate([before, own, after], axis=2)
        real, imag = cross_pass(packed[0], packed[1], taps)
    real, imag = along_pass(real, imag, taps)
    return jnp.stack([real, imag])


def solution(mesh):
    in_specs = (P("illum", None), P(), P(None, "tile", "illum"), P())
    out_specs = P(None, "illum", "tile", None)
    return jax.shard_map(body, mesh=mesh, in_specs=in_specs, out_specs=out_specs, check_vma=False)
```

```python
import jax
import jax.numpy as jnp
from jax import lax
from jax.sharding import PartitionSpec as P

NY = 4096
PLANES = 2
HALF = 16


two_pi = 6.283185307179586


def extended(cells, sides, width):
    for axis, dim in sides:
        count = lax.axis_size(axis)
        odd = lax.axis_index(axis) % 2 == 1
        head = lax.slice_in_dim(cells, 0, width, axis=dim)
        tail = lax.slice_in_dim(cells, cells.shape[dim] - width, cells.shape[dim], axis=dim)
        across = [(i, i + 1) for i in range(1, count - 1, 2)] + [(i + 1, i) for i in range(1, count - 1, 2)]
        within = [(i, i + 1) for i in range(0, count - 1, 2)] + [(i + 1, i) for i in range(0, count - 1, 2)]
        got_within = lax.ppermute(jnp.where(odd, head, tail), axis, within)
        got_across = lax.ppermute(jnp.where(odd, tail, head), axis, across)
        before = jnp.where(odd, got_within, got_across)
        after = jnp.where(odd, got_across, got_within)
        cells = jnp.concatenate([before, cells, after], axis=dim)
    return cells


def toeplitz(tap_row, block):
    rows = jnp.arange(block + 2 * HALF)[:, None]
    cols = jnp.arange(block)[None, :]
    offset = rows - cols
    steps = jnp.arange(2 * HALF + 1)
    return jnp.sum(jnp.where(offset[:, :, None] == steps, tap_row, 0.0), axis=2)


def band_matrix(tap_row, count):
    rows = jnp.arange(count)[:, None]
    cols = jnp.arange(count + 2 * HALF)[None, :]
    offset = cols - rows
    steps = jnp.arange(2 * HALF + 1)
    return jnp.sum(jnp.where(offset[:, :, None] == steps, tap_row, 0.0), axis=2)


def windows(field, block):
    length = field.shape[-1]
    count = length // block
    widths = [(0, 0)] * (field.ndim - 1) + [(HALF, block - HALF)]
    padded = jnp.pad(field, widths)
    lead = field.shape[:-1]
    main = padded[..., :length].reshape(lead + (count, block))
    after = padded[..., block : length + block].reshape(lead + (count, block))[..., : 2 * HALF]
    return jnp.concatenate([main, after], axis=-1)


def complex_stack(real_part, imag_part):
    top = jnp.concatenate([real_part, -imag_part], axis=1)
    bottom = jnp.concatenate([imag_part, real_part], axis=1)
    return jnp.concatenate([top, bottom], axis=0)


def along_pass(real, imag, taps):
    block = min(128, real.shape[-1])
    win = jnp.concatenate([windows(real, block), windows(imag, block)], axis=-1)
    kern = complex_stack(toeplitz(taps[0], block), -toeplitz(taps[1], block))
    out = jnp.einsum("...nj,jc->...nc", win, kern, precision=lax.Precision.HIGH)
    return out[..., :block].reshape(real.shape), out[..., block:].reshape(real.shape)


def cross_pass(real, imag, taps):
    count = real.shape[1] - 2 * HALF
    band = complex_stack(band_matrix(taps[0], count), band_matrix(taps[1], count))
    field = jnp.concatenate([real, imag], axis=1)
    out = jnp.einsum("ij,ajy->aiy", band, field, precision=lax.Precision.HIGH)
    return out[:, :count], out[:, count:]


def transmit(real, imag, screen):
    return rotate(real, imag, jnp.cos(screen), jnp.sin(screen))


def rotate(real, imag, cosine, sine):
    return (real * cosine - imag * sine, real * sine + imag * cosine)


def reorder(gathered, owner):
    count = gathered.shape[1]
    blocks = owner.shape[1]
    width = gathered.shape[2] // blocks
    planes = [
        gathered[p].reshape(count, blocks, width)[:, owner[p], :].reshape(count, blocks * width)
        for p in range(gathered.shape[0])
    ]
    return jnp.stack(planes)


def gather_screens(stored_planes, owner, axis):
    count = lax.axis_size(axis)
    me = lax.axis_index(axis)
    paired = count & (count - 1) == 0

    def partner(i, k):
        return i ^ k if paired else (i + k) % count

    def exchange(x, k):
        return lax.ppermute(x, axis, [(i, partner(i, k)) for i in range(count)])

    if count == 8:
        one, two, four = (exchange(stored_planes, k) for k in (1, 2, 4))
        three, six = exchange(jnp.stack([one, four]), 2)
        five = exchange(four, 1)
        seven = exchange(four, 3)
        parts = [stored_planes, one, two, three, four, five, six, seven]
        first = [three, six, seven]
    else:
        parts = [stored_planes] + [exchange(stored_planes, k) for k in range(1, count)]
        first = parts[1:]
    landed = sum(part[0, 0, 0] for part in first) * 0.0
    stacked = jnp.stack(parts, axis=1)
    rows = stored_planes.shape[1]
    width = stored_planes.shape[2]
    planes = []
    for p in range(stored_planes.shape[0]):
        source = jnp.bitwise_xor(me, owner[p]) if paired else jnp.mod(me - owner[p], count)
        picked = stacked[p][source]
        planes.append(jnp.transpose(picked, (1, 0, 2)).reshape(rows, count * width))
    return jnp.stack(planes), landed


def body(tilts, taps, stored_planes, owner):
    local_rows = stored_planes.shape[1]
    total_rows = local_rows * lax.axis_size("tile")
    total_cols = NY
    first_row = lax.axis_index("tile") * local_rows
    screens, landed = gather_screens(stored_planes, owner, "illum")
    taps = taps + landed
    extra = HALF
    span = local_rows + 2 * extra
    global_rows = first_row - extra + jnp.arange(span, dtype=jnp.int32)
    inside = (global_rows >= 0) & (global_rows < total_rows)
    cols = jnp.arange(total_cols, dtype=jnp.int32)
    across = (
        jnp.mod(tilts[:, 0:1] * global_rows[None, :], total_rows).astype(jnp.float32) / total_rows
    )
    along = jnp.mod(tilts[:, 1:2] * cols[None, :], total_cols).astype(jnp.float32) / total_cols
    across_cos = jnp.where(inside[None, :], jnp.cos(two_pi * across), 0.0)[:, :, None]
    across_sin = jnp.where(inside[None, :], jnp.sin(two_pi * across), 0.0)[:, :, None]
    along_cos = jnp.cos(two_pi * along)[:, None, :]
    along_sin = jnp.sin(two_pi * along)[:, None, :]

    def incident(rows):
        real = across_cos[:, rows] * along_cos - across_sin[:, rows] * along_sin
        imag = across_sin[:, rows] * along_cos + across_cos[:, rows] * along_sin
        return real, imag

    halo = extended(screens[0], (("tile", 0),), HALF)
    pieces = [
        transmit(*incident(rows), screen)
        for rows, screen in (
            (slice(0, HALF), halo[:HALF]),
            (slice(HALF, HALF + local_rows), screens[0]),
            (slice(HALF + local_rows, span), halo[HALF + local_rows :]),
        )
    ]
    real = jnp.concatenate([piece[0] for piece in pieces], axis=1)
    imag = jnp.concatenate([piece[1] for piece in pieces], axis=1)
    real, imag = cross_pass(real, imag, taps)
    real, imag = along_pass(real, imag, taps)
    for plane in range(1, PLANES):
        real, imag = transmit(real, imag, screens[plane])
        packed = extended(jnp.stack([real, imag]), (("tile", 2),), HALF)
        real, imag = cross_pass(packed[0], packed[1], taps)
        real, imag = along_pass(real, imag, taps)
    return jnp.stack([real, imag])


def solution(mesh):
    in_specs = (P("illum", None), P(), P(None, "tile", "illum"), P())
    out_specs = P(None, "illum", "tile", None)
    return jax.shard_map(body, mesh=mesh, in_specs=in_specs, out_specs=out_specs, check_vma=False)
```

```python
import jax
import jax.numpy as jnp
from jax import lax
from jax.sharding import PartitionSpec as P

NY = 4096
PLANES = 2
HALF = 16


two_pi = 6.283185307179586


def extended(cells, sides, width):
    for axis, dim in sides:
        count = lax.axis_size(axis)
        odd = lax.axis_index(axis) % 2 == 1
        head = lax.slice_in_dim(cells, 0, width, axis=dim)
        tail = lax.slice_in_dim(cells, cells.shape[dim] - width, cells.shape[dim], axis=dim)
        across = [(i, i + 1) for i in range(1, count - 1, 2)] + [(i + 1, i) for i in range(1, count - 1, 2)]
        within = [(i, i + 1) for i in range(0, count - 1, 2)] + [(i + 1, i) for i in range(0, count - 1, 2)]
        got_within = lax.ppermute(jnp.where(odd, head, tail), axis, within)
        got_across = lax.ppermute(jnp.where(odd, tail, head), axis, across)
        cells = jnp.concatenate([got_within, cells, got_across], axis=dim)
    return cells


def toeplitz(tap_row, block):
    rows = jnp.arange(block + 2 * HALF)[:, None]
    cols = jnp.arange(block)[None, :]
    offset = rows - cols
    steps = jnp.arange(2 * HALF + 1)
    return jnp.sum(jnp.where(offset[:, :, None] == steps, tap_row, 0.0), axis=2)


def band_matrix(tap_row, count):
    rows = jnp.arange(count)[:, None]
    cols = jnp.arange(count + 2 * HALF)[None, :]
    offset = cols - rows
    steps = jnp.arange(2 * HALF + 1)
    return jnp.sum(jnp.where(offset[:, :, None] == steps, tap_row, 0.0), axis=2)


def windows(field, block):
    length = field.shape[-1]
    count = length // block
    widths = [(0, 0)] * (field.ndim - 1) + [(HALF, block - HALF)]
    padded = jnp.pad(field, widths)
    lead = field.shape[:-1]
    main = padded[..., :length].reshape(lead + (count, block))
    after = padded[..., block : length + block].reshape(lead + (count, block))[..., : 2 * HALF]
    return jnp.concatenate([main, after], axis=-1)


def complex_stack(real_part, imag_part):
    top = jnp.concatenate([real_part, -imag_part], axis=1)
    bottom = jnp.concatenate([imag_part, real_part], axis=1)
    return jnp.concatenate([top, bottom], axis=0)


def along_pass(real, imag, taps):
    block = min(128, real.shape[-1])
    win = jnp.concatenate([windows(real, block), windows(imag, block)], axis=-1)
    kern = complex_stack(toeplitz(taps[0], block), -toeplitz(taps[1], block))
    out = jnp.einsum("...nj,jc->...nc", win, kern, precision=lax.Precision.HIGH)
    return out[..., :block].reshape(real.shape), out[..., block:].reshape(real.shape)


def cross_pass(real, imag, taps, odd):
    count = real.shape[1] - 2 * HALF

    def placed(band):
        swapped = jnp.concatenate([band[:, HALF + count :], band[:, HALF : HALF + count], band[:, :HALF]], axis=1)
        return jnp.where(odd, band, swapped)

    band = complex_stack(placed(band_matrix(taps[0], count)), placed(band_matrix(taps[1], count)))
    field = jnp.concatenate([real, imag], axis=1)
    out = jnp.einsum("ij,ajy->aiy", band, field, precision=lax.Precision.HIGH)
    return out[:, :count], out[:, count:]


def transmit(real, imag, screen):
    return rotate(real, imag, jnp.cos(screen), jnp.sin(screen))


def rotate(real, imag, cosine, sine):
    return (real * cosine - imag * sine, real * sine + imag * cosine)


def reorder(gathered, owner):
    count = gathered.shape[1]
    blocks = owner.shape[1]
    width = gathered.shape[2] // blocks
    planes = [
        gathered[p].reshape(count, blocks, width)[:, owner[p], :].reshape(count, blocks * width)
        for p in range(gathered.shape[0])
    ]
    return jnp.stack(planes)


def gather_screens(stored_planes, owner, axis):
    count = lax.axis_size(axis)
    me = lax.axis_index(axis)
    paired = count & (count - 1) == 0

    def partner(i, k):
        return i ^ k if paired else (i + k) % count

    def exchange(x, k):
        return lax.ppermute(x, axis, [(i, partner(i, k)) for i in range(count)])

    if count == 8:
        one, two, four = (exchange(stored_planes, k) for k in (1, 2, 4))
        three, five = exchange(jnp.stack([two, four]), 1)
        six = exchange(four, 2)
        seven = exchange(four, 3)
        parts = [stored_planes, one, two, three, four, five, six, seven]
        first = [three, six, seven]
    else:
        parts = [stored_planes] + [exchange(stored_planes, k) for k in range(1, count)]
        first = parts[1:]
    landed = sum(part[0, 0, 0] for part in first) * 0.0
    stacked = jnp.stack(parts, axis=1)
    rows = stored_planes.shape[1]
    width = stored_planes.shape[2]
    planes = []
    for p in range(stored_planes.shape[0]):
        source = jnp.bitwise_xor(me, owner[p]) if paired else jnp.mod(me - owner[p], count)
        picked = stacked[p][source]
        planes.append(jnp.transpose(picked, (1, 0, 2)).reshape(rows, count * width))
    return jnp.stack(planes), landed


def body(tilts, taps, stored_planes, owner):
    local_rows = stored_planes.shape[1]
    total_rows = local_rows * lax.axis_size("tile")
    total_cols = NY
    first_row = lax.axis_index("tile") * local_rows
    screens, landed = gather_screens(stored_planes, owner, "illum")
    taps = taps + landed
    extra = HALF
    span = local_rows + 2 * extra
    global_rows = first_row - extra + jnp.arange(span, dtype=jnp.int32)
    inside = (global_rows >= 0) & (global_rows < total_rows)
    cols = jnp.arange(total_cols, dtype=jnp.int32)
    across = (
        jnp.mod(tilts[:, 0:1] * global_rows[None, :], total_rows).astype(jnp.float32) / total_rows
    )
    along = jnp.mod(tilts[:, 1:2] * cols[None, :], total_cols).astype(jnp.float32) / total_cols
    across_cos = jnp.where(inside[None, :], jnp.cos(two_pi * across), 0.0)[:, :, None]
    across_sin = jnp.where(inside[None, :], jnp.sin(two_pi * across), 0.0)[:, :, None]
    along_cos = jnp.cos(two_pi * along)[:, None, :]
    along_sin = jnp.sin(two_pi * along)[:, None, :]

    odd = lax.axis_index("tile") % 2 == 1

    def incident(rows, other=None):
        a_cos, a_sin = across_cos[:, rows], across_sin[:, rows]
        if other is not None:
            a_cos = jnp.where(odd, a_cos, across_cos[:, other])
            a_sin = jnp.where(odd, a_sin, across_sin[:, other])
        real = a_cos * along_cos - a_sin * along_sin
        imag = a_sin * along_cos + a_cos * along_sin
        return real, imag

    halo = extended(screens[0], (("tile", 0),), HALF)
    pieces = [
        transmit(*incident(*rows), screen)
        for rows, screen in (
            ((slice(0, HALF), slice(HALF + local_rows, span)), halo[:HALF]),
            ((slice(HALF, HALF + local_rows),), screens[0]),
            ((slice(HALF + local_rows, span), slice(0, HALF)), halo[HALF + local_rows :]),
        )
    ]
    real = jnp.concatenate([piece[0] for piece in pieces], axis=1)
    imag = jnp.concatenate([piece[1] for piece in pieces], axis=1)
    real, imag = cross_pass(real, imag, taps, odd)
    real, imag = along_pass(real, imag, taps)
    for plane in range(1, PLANES):
        real, imag = transmit(real, imag, screens[plane])
        packed = extended(jnp.stack([real, imag]), (("tile", 2),), HALF)
        real, imag = cross_pass(packed[0], packed[1], taps, odd)
        real, imag = along_pass(real, imag, taps)
    return jnp.stack([real, imag])


def solution(mesh):
    in_specs = (P("illum", None), P(), P(None, "tile", "illum"), P())
    out_specs = P(None, "illum", "tile", None)
    return jax.shard_map(body, mesh=mesh, in_specs=in_specs, out_specs=out_specs, check_vma=False)
```
